32 devices in a mesh: cell: 16 (over z, y, core), bin: 2 (over x).
Axes of the slice: x: 2, y: 2, z: 4, core: 2. Of those that a mesh axis runs over, the one named last changes fastest.
Arguments:
- tensor: float32 [96, 4096, 1024], P('cell', None, 'bin'), may hold values from -6 to 6
- cell_factor: float32 [4096, 128], P('cell'), may hold values from -4 to 4
- bin_factor: float32 [1024, 128], P('bin'), may hold values from -4 to 4
Outputs:
- updated: float32 [96, 128], P('cell', 'bin')
The draws below stay inside these ranges and needn't reach their ends.
All inputs are finite; a program needn't handle non-finite values.
Results may differ from the reference program's by a relative error of at most 0.000096.
Values sent between devices are 32-bit elements; how exact they have to be, the bound alone decides.
No kernel may reach another device: no remote copies, remote signals or barrier semaphores. Data moves between devices by JAX's collectives and lax.ppermute only.
A program may use at most 128 MiB of HBM per device.

```python
import jax
import jax.numpy as jnp
from jax import lax

J = 4096
K = 1024
R = 128
IMAGES = 96


def factor_draw(key, rowcount, colcount):
    key_common, key_noise, key_scale = jax.random.split(key, 3)
    common = jnp.clip(jax.random.normal(key_common, (rowcount, 1), jnp.float32), -4.0, 4.0)
    noise = jnp.clip(jax.random.normal(key_noise, (rowcount, colcount), jnp.float32), -4.0, 4.0)
    ramp = 1.0 + 2.0 * jnp.arange(rowcount, dtype=jnp.float32) / (rowcount - 1)
    jitter = jnp.exp(jax.random.uniform(key_scale, (rowcount, 1), jnp.float32, -0.35, 0.35))
    scaling = ramp[:, None] * jitter / (2.0 * rowcount ** 0.5)
    return (scaling * (0.6 * common + 0.8 * noise)).astype(jnp.float32)


def draw_cell_factor(key, part):
    return factor_draw(jax.random.fold_in(key, 11), J, R)


def draw_bin_factor(key, part):
    return factor_draw(jax.random.fold_in(key, 23), K, R)


def block_levels(rng, dims, pieces, smallest, top_value):
    factor_of = 1.0
    for axis_at, shards_of in pieces:
        heights = jax.random.uniform(jax.random.fold_in(jax.random.fold_in(rng, 6), axis_at), (shards_of,), jnp.float32, smallest / len(pieces), top_value / len(pieces))
        factor_of = factor_of * jnp.repeat(jnp.exp(heights), dims[axis_at] // shards_of).reshape((-1,) + (1,) * (len(dims) - 1 - axis_at))
    return factor_of


def bell_draw(stream_key, dims, deviation, reach, shards=(), kind=jnp.bfloat16):
    drawn = deviation * jax.random.normal(stream_key, dims, jnp.float32)
    if shards:
        drawn = drawn * block_levels(stream_key, dims, shards, -0.22, 0.18)
    return jnp.clip(drawn, -reach, reach).astype(kind)


def setup_inputs(seed: int = 0) -> dict:
    seeds = jax.random.split(jax.random.key(seed), 4)
    tensor = bell_draw(seeds[0], (IMAGES, J, K), 1.0, 6.0, ((0, 16), (2, 2)), jnp.float32)
    cell_factor = draw_cell_factor(jax.random.fold_in(seeds[3], 71), 0)
    bin_factor = draw_bin_factor(jax.random.fold_in(seeds[3], 71), 0)
    return dict(tensor=tensor, cell_factor=cell_factor, bin_factor=bin_factor)


def reference(tensor, cell_factor, bin_factor):
    highest = lax.Precision.HIGHEST
    projected = jnp.einsum('ijk,kr->ijr', tensor, bin_factor, precision=highest)
    mttkrp = jnp.einsum('ijr,jr->ir', projected, cell_factor, precision=highest)
    gram_cell = jnp.dot(cell_factor.T, cell_factor, precision=highest)
    gram_bin = jnp.dot(bin_factor.T, bin_factor, precision=highest)
    gram = gram_cell * gram_bin
    chol_lower = jnp.linalg.cholesky(gram)
    return jax.scipy.linalg.cho_solve((chol_lower, True), mttkrp.T).T
```

```python
import jax
import jax.numpy as jnp
from jax import lax
from jax.sharding import PartitionSpec as P


def exchange_sum(value, axis):
    size = lax.axis_size(axis)
    stride = 1
    while stride < size:
        pairs = [(i, i ^ stride) for i in range(size)]
        value = value + lax.ppermute(value, axis, pairs)
        stride *= 2
    return value


def body(tensor, cell_factor, bin_factor):
    highest = lax.Precision.HIGHEST
    image_rows, cell_count, bin_count = tensor.shape
    rank_cols = bin_factor.shape[1]
    cell_full = lax.all_gather(cell_factor, "cell", axis=0, tiled=True)
    gram_bin = exchange_sum(jnp.dot(bin_factor.T, bin_factor, precision=highest), "bin")
    projected = jnp.dot(
        tensor.reshape(image_rows * cell_count, bin_count), bin_factor, precision=highest
    )
    projected = projected.reshape(image_rows, cell_count, rank_cols)
    mttkrp = jnp.sum(projected * cell_full[None, :, :], axis=1)
    gram_cell = jnp.dot(cell_full.T, cell_full, precision=highest)
    gram = gram_cell * gram_bin
    chol_lower = jnp.linalg.cholesky(gram)
    totals = exchange_sum(mttkrp, "bin")
    solved = jax.scipy.linalg.cho_solve((chol_lower, True), totals.T).T
    own_cols = rank_cols // lax.axis_size("bin")
    updated = lax.dynamic_slice_in_dim(solved, lax.axis_index("bin") * own_cols, own_cols, 1)
    return updated


def solution(mesh):
    placed = (P("cell", None, "bin"), P("cell", None), P("bin", None))
    return jax.shard_map(
        body, mesh=mesh, in_specs=placed, out_specs=P("cell", "bin"), check_vma=False
    )
```

```python
import jax
import jax.numpy as jnp
from jax import lax
from jax.experimental import pallas as pl
from jax.experimental.pallas import tpu as pltpu
from jax.sharding import PartitionSpec as P


def exchange_sum(value, axis):
    size = lax.axis_size(axis)
    stride = 1
    while stride < size:
        pairs = [(i, i ^ stride) for i in range(size)]
        value = value + lax.ppermute(value, axis, pairs)
        stride *= 2
    return value


def split_pair(x):
    scaled = x * 65537.0
    hi = scaled - (scaled - x)
    lo = x - hi
    return hi.astype(jnp.bfloat16), lo.astype(jnp.bfloat16)


def gram_of(x):
    hi, lo = split_pair(x)
    both = jnp.concatenate([hi, lo], axis=1)
    full = lax.dot_general(
        both, both, (((0,), (0,)), ((), ())), preferred_element_type=jnp.float32
    )
    n = x.shape[1]
    return (full[:n, :n] + full[n:, n:]) + (full[:n, n:] + full[n:, :n])


def project_kernel(t_ref, b_ref, o_ref):
    rank_cols = o_ref.shape[1]
    hi, lo = split_pair(t_ref[...])
    pair = b_ref[...]
    acc = jnp.dot(hi, pair, preferred_element_type=jnp.float32)
    acc = acc + jnp.dot(lo, pair, preferred_element_type=jnp.float32)
    o_ref[...] = acc[:, :rank_cols] + acc[:, rank_cols:]


def project(flat, bin_factor, block_rows=1024):
    rows, bin_count = flat.shape
    rank_cols = bin_factor.shape[1]
    b_hi, b_lo = split_pair(bin_factor)
    pair = jnp.concatenate([b_hi, b_lo], axis=1)
    return pl.pallas_call(
        project_kernel,
        out_shape=jax.ShapeDtypeStruct((rows, rank_cols), jnp.float32),
        grid=(rows // block_rows,),
        in_specs=[
            pl.BlockSpec((block_rows, bin_count), lambda i: (i, 0)),
            pl.BlockSpec((bin_count, 2 * rank_cols), lambda i: (0, 0)),
        ],
        out_specs=pl.BlockSpec((block_rows, rank_cols), lambda i: (i, 0)),
        cost_estimate=pl.CostEstimate(
            flops=8 * rows * bin_count * rank_cols,
            transcendentals=0,
            bytes_accessed=4 * rows * (bin_count + rank_cols),
        ),
    )(flat, pair)


def body(tensor, cell_factor, bin_factor):
    image_rows, cell_count, bin_count = tensor.shape
    rank_cols = bin_factor.shape[1]
    cell_full = lax.all_gather(cell_factor, "cell", axis=0, tiled=True)
    gram_bin = exchange_sum(gram_of(bin_factor), "bin")
    projected = project(tensor.reshape(image_rows * cell_count, bin_count), bin_factor)
    projected = projected.reshape(image_rows, cell_count, rank_cols)
    mttkrp = jnp.sum(projected * cell_full[None, :, :], axis=1)
    gram = gram_of(cell_full) * gram_bin
    chol_lower = jnp.linalg.cholesky(gram)
    totals = exchange_sum(mttkrp, "bin")
    solved = jax.scipy.linalg.cho_solve((chol_lower, True), totals.T).T
    own_cols = rank_cols // lax.axis_size("bin")
    updated = lax.dynamic_slice_in_dim(solved, lax.axis_index("bin") * own_cols, own_cols, 1)
    return updated


def solution(mesh):
    placed = (P("cell", None, "bin"), P("cell", None), P("bin", None))
    return jax.shard_map(
        body, mesh=mesh, in_specs=placed, out_specs=P("cell", "bin"), check_vma=False
    )
```

```python
import jax
import jax.numpy as jnp
from jax import lax
from jax.experimental import pallas as pl
from jax.experimental.pallas import tpu as pltpu
from jax.sharding import PartitionSpec as P


def exchange_sum(value, axis):
    size = lax.axis_size(axis)
    stride = 1
    while stride < size:
        pairs = [(i, i ^ stride) for i in range(size)]
        value = value + lax.ppermute(value, axis, pairs)
        stride *= 2
    return value


def split_pair(x):
    scaled = x * 65537.0
    hi = scaled - (scaled - x)
    lo = x - hi
    return hi.astype(jnp.bfloat16), lo.astype(jnp.bfloat16)


def gram_of(x):
    hi, lo = split_pair(x)
    both = jnp.concatenate([hi, lo], axis=1)
    full = lax.dot_general(
        both, both, (((0,), (0,)), ((), ())), preferred_element_type=jnp.float32
    )
    n = x.shape[1]
    return (full[:n, :n] + full[n:, n:]) + (full[:n, n:] + full[n:, :n])


def project_kernel(t_ref, b_ref, o_ref):
    rank_cols = o_ref.shape[1]
    hi, lo = split_pair(t_ref[...])
    pair = b_ref[...]
    acc = jnp.dot(hi, pair, preferred_element_type=jnp.float32)
    acc = acc + jnp.dot(lo, pair, preferred_element_type=jnp.float32)
    o_ref[...] = acc[:, :rank_cols] + acc[:, rank_cols:]


def project(flat, bin_factor, block_rows=1024):
    rows, bin_count = flat.shape
    rank_cols = bin_factor.shape[1]
    b_hi, b_lo = split_pair(bin_factor)
    pair = jnp.concatenate([b_hi, b_lo], axis=1)
    return pl.pallas_call(
        project_kernel,
        out_shape=jax.ShapeDtypeStruct((rows, rank_cols), jnp.float32),
        grid=(rows // block_rows,),
        in_specs=[
            pl.BlockSpec((block_rows, bin_count), lambda i: (i, 0)),
            pl.BlockSpec((bin_count, 2 * rank_cols), lambda i: (0, 0)),
        ],
        out_specs=pl.BlockSpec((block_rows, rank_cols), lambda i: (i, 0)),
        cost_estimate=pl.CostEstimate(
            flops=8 * rows * bin_count * rank_cols,
            transcendentals=0,
            bytes_accessed=4 * rows * (bin_count + rank_cols),
        ),
    )(flat, pair)


def body(tensor, cell_factor, bin_factor):
    image_rows, cell_count, bin_count = tensor.shape
    rank_cols = bin_factor.shape[1]
    cell_size = lax.axis_size("cell")
    spread = jnp.broadcast_to(cell_factor[None], (cell_size,) + cell_factor.shape)
    cell_full = lax.all_to_all(spread, "cell", 0, 0, tiled=True).reshape(-1, rank_cols)
    gram_bin = exchange_sum(gram_of(bin_factor), "bin")
    projected = project(tensor.reshape(image_rows * cell_count, bin_count), bin_factor)
    projected = projected.reshape(image_rows, cell_count, rank_cols)
    mttkrp = jnp.sum(projected * cell_full[None, :, :], axis=1)
    gram = gram_of(cell_full) * gram_bin
    chol_lower = jnp.linalg.cholesky(gram)
    totals = exchange_sum(mttkrp, "bin")
    solved = jax.scipy.linalg.cho_solve((chol_lower, True), totals.T).T
    own_cols = rank_cols // lax.axis_size("bin")
    updated = lax.dynamic_slice_in_dim(solved, lax.axis_index("bin") * own_cols, own_cols, 1)
    return updated


def solution(mesh):
    placed = (P("cell", None, "bin"), P("cell", None), P("bin", None))
    return jax.shard_map(
        body, mesh=mesh, in_specs=placed, out_specs=P("cell", "bin"), check_vma=False
    )
```

```python
import jax
import jax.numpy as jnp
from jax import lax
from jax.experimental import pallas as pl
from jax.experimental.pallas import tpu as pltpu
from jax.sharding import PartitionSpec as P


def exchange_sum(value, axis):
    size = lax.axis_size(axis)
    stride = 1
    while stride < size:
        pairs = [(i, i ^ stride) for i in range(size)]
        value = value + lax.ppermute(value, axis, pairs)
        stride *= 2
    return value


def split_pair(x):
    scaled = x * 65537.0
    hi = scaled - (scaled - x)
    lo = x - hi
    return hi.astype(jnp.bfloat16), lo.astype(jnp.bfloat16)


def gram_of(x):
    hi, lo = split_pair(x)
    both = jnp.concatenate([hi, lo], axis=1)
    full = lax.dot_general(
        both, both, (((0,), (0,)), ((), ())), preferred_element_type=jnp.float32
    )
    n = x.shape[1]
    return (full[:n, :n] + full[n:, n:]) + (full[:n, n:] + full[n:, :n])


def project_kernel(t_ref, b_ref, o_ref):
    rank_cols = o_ref.shape[1]
    hi, lo = split_pair(t_ref[...])
    pair = b_ref[...]
    acc = jnp.dot(hi, pair, preferred_element_type=jnp.float32)
    acc = acc + jnp.dot(lo, pair, preferred_element_type=jnp.float32)
    o_ref[...] = acc[:, :rank_cols] + acc[:, rank_cols:]


def project(flat, bin_factor, block_rows=4096):
    rows, bin_count = flat.shape
    rank_cols = bin_factor.shape[1]
    b_hi, b_lo = split_pair(bin_factor)
    pair = jnp.concatenate([b_hi, b_lo], axis=1)
    return pl.pallas_call(
        project_kernel,
        out_shape=jax.ShapeDtypeStruct((rows, rank_cols), jnp.float32),
        grid=(rows // block_rows,),
        in_specs=[
            pl.BlockSpec((block_rows, bin_count), lambda i: (i, 0)),
            pl.BlockSpec((bin_count, 2 * rank_cols), lambda i: (0, 0)),
        ],
        out_specs=pl.BlockSpec((block_rows, rank_cols), lambda i: (i, 0)),
        cost_estimate=pl.CostEstimate(
            flops=8 * rows * bin_count * rank_cols,
            transcendentals=0,
            bytes_accessed=4 * rows * (bin_count + rank_cols),
        ),
    )(flat, pair)


def body(tensor, cell_factor, bin_factor):
    image_rows, cell_count, bin_count = tensor.shape
    rank_cols = bin_factor.shape[1]
    cell_size = lax.axis_size("cell")
    spread = jnp.broadcast_to(cell_factor[None], (cell_size,) + cell_factor.shape)
    cell_full = lax.all_to_all(spread, "cell", 0, 0, tiled=True).reshape(-1, rank_cols)
    gram_bin = exchange_sum(gram_of(bin_factor), "bin")
    projected = project(tensor.reshape(image_rows * cell_count, bin_count), bin_factor)
    projected = projected.reshape(image_rows, cell_count, rank_cols)
    mttkrp = jnp.sum(projected * cell_full[None, :, :], axis=1)
    gram = gram_of(cell_full) * gram_bin
    chol_lower = jnp.linalg.cholesky(gram)
    totals = exchange_sum(mttkrp, "bin")
    solved = jax.scipy.linalg.cho_solve((chol_lower, True), totals.T).T
    own_cols = rank_cols // lax.axis_size("bin")
    updated = lax.dynamic_slice_in_dim(solved, lax.axis_index("bin") * own_cols, own_cols, 1)
    return updated


def solution(mesh):
    placed = (P("cell", None, "bin"), P("cell", None), P("bin", None))
    return jax.shard_map(
        body, mesh=mesh, in_specs=placed, out_specs=P("cell", "bin"), check_vma=False
    )
```

```python
import jax
import jax.numpy as jnp
from jax import lax
from jax.experimental import pallas as pl
from jax.experimental.pallas import tpu as pltpu
from jax.sharding import Mesh, PartitionSpec as P


def exchange_sum(value, axis):
    size = lax.axis_size(axis)
    stride = 1
    while stride < size:
        pairs = [(i, i ^ stride) for i in range(size)]
        value = value + lax.ppermute(value, axis, pairs)
        stride *= 2
    return value


def split_pair(x):
    scaled = x * 65537.0
    hi = scaled - (scaled - x)
    lo = x - hi
    return hi.astype(jnp.bfloat16), lo.astype(jnp.bfloat16)


def gram_of(x):
    hi, lo = split_pair(x)
    both = jnp.concatenate([hi, lo], axis=1)
    full = lax.dot_general(
        both, both, (((0,), (0,)), ((), ())), preferred_element_type=jnp.float32
    )
    n = x.shape[1]
    return (full[:n, :n] + full[n:, n:]) + (full[:n, n:] + full[n:, :n])


def project_kernel(t_ref, b_ref, o_ref):
    rank_cols = o_ref.shape[1]
    hi, lo = split_pair(t_ref[...])
    pair = b_ref[...]
    acc = jnp.dot(hi, pair, preferred_element_type=jnp.float32)
    acc = acc + jnp.dot(lo, pair, preferred_element_type=jnp.float32)
    o_ref[...] = acc[:, :rank_cols] + acc[:, rank_cols:]


def project(flat, bin_factor, first_row, rows, block_rows=4096):
    bin_count = flat.shape[1]
    start = first_row // block_rows
    rank_cols = bin_factor.shape[1]
    b_hi, b_lo = split_pair(bin_factor)
    pair = jnp.concatenate([b_hi, b_lo], axis=1)
    return pl.pallas_call(
        project_kernel,
        out_shape=jax.ShapeDtypeStruct((rows, rank_cols), jnp.float32),
        grid=(rows // block_rows,),
        in_specs=[
            pl.BlockSpec((block_rows, bin_count), lambda i: (i + start, 0)),
            pl.BlockSpec((bin_count, 2 * rank_cols), lambda i: (0, 0)),
        ],
        out_specs=pl.BlockSpec((block_rows, rank_cols), lambda i: (i, 0)),
        cost_estimate=pl.CostEstimate(
            flops=8 * rows * bin_count * rank_cols,
            transcendentals=0,
            bytes_accessed=4 * rows * (bin_count + rank_cols),
        ),
    )(flat, pair)


def gather_cells(cell_factor, project_first):
    outer = lax.axis_size("cell_outer")
    spread = jnp.broadcast_to(cell_factor[None], (outer,) + cell_factor.shape)
    mine = lax.all_to_all(spread, "cell_outer", 0, 0, tiled=True)
    mine, first_part = lax.optimization_barrier((mine, project_first()))
    core_count = lax.axis_size("cell_core")
    if core_count == 1:
        return mine.reshape(-1, cell_factor.shape[1]), first_part
    other = lax.ppermute(mine, "cell_core", [(0, 1), (1, 0)])
    first = lax.axis_index("cell_core") == 0
    pair = (jnp.where(first, mine, other), jnp.where(first, other, mine))
    return jnp.stack(pair, axis=1).reshape(-1, cell_factor.shape[1]), first_part


def body(tensor, cell_factor, bin_factor):
    image_rows, cell_count, bin_count = tensor.shape
    rank_cols = bin_factor.shape[1]
    half = image_rows // 2
    flat = tensor.reshape(image_rows * cell_count, bin_count)
    cell_full, first_part = gather_cells(
        cell_factor, lambda: project(flat, bin_factor, 0, half * cell_count)
    )
    gram_bin = exchange_sum(gram_of(bin_factor), "bin")
    second_part = project(
        flat, bin_factor, half * cell_count, (image_rows - half) * cell_count
    )
    projected = jnp.concatenate([first_part, second_part], axis=0)
    projected = projected.reshape(image_rows, cell_count, rank_cols)
    mttkrp = jnp.sum(projected * cell_full[None, :, :], axis=1)
    gram = gram_of(cell_full) * gram_bin
    chol_lower = jnp.linalg.cholesky(gram)
    totals = exchange_sum(mttkrp, "bin")
    solved = jax.scipy.linalg.cho_solve((chol_lower, True), totals.T).T
    own_cols = rank_cols // lax.axis_size("bin")
    updated = lax.dynamic_slice_in_dim(solved, lax.axis_index("bin") * own_cols, own_cols, 1)
    return updated


def solution(mesh):
    cell_size, bin_size = mesh.shape["cell"], mesh.shape["bin"]
    core_count = 2 if cell_size % 2 == 0 else 1
    split = Mesh(
        mesh.devices.reshape(cell_size // core_count, core_count, bin_size),
        ("cell_outer", "cell_core", "bin"),
    )
    cell = ("cell_outer", "cell_core")
    placed = (P(cell, None, "bin"), P(cell, None), P("bin", None))
    return jax.shard_map(
        body, mesh=split, in_specs=placed, out_specs=P(cell, "bin"), check_vma=False
    )
```

```python
import jax
import jax.numpy as jnp
from jax import lax
from jax.experimental import pallas as pl
from jax.experimental.pallas import tpu as pltpu
from jax.sharding import Mesh, PartitionSpec as P


def exchange_sum(value, axis):
    size = lax.axis_size(axis)
    stride = 1
    while stride < size:
        pairs = [(i, i ^ stride) for i in range(size)]
        value = value + lax.ppermute(value, axis, pairs)
        stride *= 2
    return value


def split_pair(x):
    scaled = x * 65537.0
    hi = scaled - (scaled - x)
    lo = x - hi
    return hi.astype(jnp.bfloat16), lo.astype(jnp.bfloat16)


def gram_of(x):
    hi, lo = split_pair(x)
    both = jnp.concatenate([hi, lo], axis=1)
    full = lax.dot_general(
        both, both, (((0,), (0,)), ((), ())), preferred_element_type=jnp.float32
    )
    n = x.shape[1]
    return (full[:n, :n] + full[n:, n:]) + (full[:n, n:] + full[n:, :n])


def project_kernel(t_ref, b_ref, o_ref):
    rank_cols = o_ref.shape[1]
    hi, lo = split_pair(t_ref[...])
    pair = b_ref[...]
    acc = jnp.dot(hi, pair, preferred_element_type=jnp.float32)
    acc = acc + jnp.dot(lo, pair, preferred_element_type=jnp.float32)
    o_ref[...] = acc[:, :rank_cols] + acc[:, rank_cols:]


def project(flat, bin_factor, first_row, rows, block_rows=4096):
    bin_count = flat.shape[1]
    start = first_row // block_rows
    rank_cols = bin_factor.shape[1]
    b_hi, b_lo = split_pair(bin_factor)
    pair = jnp.concatenate([b_hi, b_lo], axis=1)
    return pl.pallas_call(
        project_kernel,
        out_shape=jax.ShapeDtypeStruct((rows, rank_cols), jnp.float32),
        grid=(rows // block_rows,),
        in_specs=[
            pl.BlockSpec((block_rows, bin_count), lambda i: (i + start, 0)),
            pl.BlockSpec((bin_count, 2 * rank_cols), lambda i: (0, 0)),
        ],
        out_specs=pl.BlockSpec((block_rows, rank_cols), lambda i: (i, 0)),
        cost_estimate=pl.CostEstimate(
            flops=8 * rows * bin_count * rank_cols,
            transcendentals=0,
            bytes_accessed=4 * rows * (bin_count + rank_cols),
        ),
    )(flat, pair)


def gather_cells(cell_factor, project_first):
    outer = lax.axis_size("cell_outer")
    spread = jnp.broadcast_to(cell_factor[None], (outer,) + cell_factor.shape)
    mine = lax.all_to_all(spread, "cell_outer", 0, 0, tiled=True)
    mine, first_part = lax.optimization_barrier((mine, project_first()))
    core_count = lax.axis_size("cell_core")
    if core_count == 1:
        return mine.reshape(-1, cell_factor.shape[1]), first_part
    other = lax.ppermute(mine, "cell_core", [(0, 1), (1, 0)])
    first = lax.axis_index("cell_core") == 0
    pair = (jnp.where(first, mine, other), jnp.where(first, other, mine))
    return jnp.stack(pair, axis=1).reshape(-1, cell_factor.shape[1]), first_part


def body(tensor, cell_factor, bin_factor):
    image_rows, cell_count, bin_count = tensor.shape
    rank_cols = bin_factor.shape[1]
    half = image_rows // 2
    flat = tensor.reshape(image_rows * cell_count, bin_count)
    cell_full, first_part = gather_cells(
        cell_factor, lambda: project(flat, bin_factor, 0, half * cell_count)
    )
    gram_bin = exchange_sum(gram_of(bin_factor), "bin")
    second_part = project(
        flat, bin_factor, half * cell_count, (image_rows - half) * cell_count
    )
    mttkrp = jnp.concatenate(
        [
            jnp.sum(part.reshape(-1, cell_count, rank_cols) * cell_full[None], axis=1)
            for part in (first_part, second_part)
        ],
        axis=0,
    )
    gram = gram_of(cell_full) * gram_bin
    chol_lower = jnp.linalg.cholesky(gram)
    totals = exchange_sum(mttkrp, "bin")
    solved = jax.scipy.linalg.cho_solve((chol_lower, True), totals.T).T
    own_cols = rank_cols // lax.axis_size("bin")
    updated = lax.dynamic_slice_in_dim(solved, lax.axis_index("bin") * own_cols, own_cols, 1)
    return updated


def solution(mesh):
    cell_size, bin_size = mesh.shape["cell"], mesh.shape["bin"]
    core_count = 2 if cell_size % 2 == 0 else 1
    split = Mesh(
        mesh.devices.reshape(cell_size // core_count, core_count, bin_size),
        ("cell_outer", "cell_core", "bin"),
    )
    cell = ("cell_outer", "cell_core")
    placed = (P(cell, None, "bin"), P(cell, None), P("bin", None))
    return jax.shard_map(
        body, mesh=split, in_specs=placed, out_specs=P(cell, "bin"), check_vma=False
    )
```

```python
import jax
import jax.numpy as jnp
from jax import lax
from jax.experimental import pallas as pl
from jax.experimental.pallas import tpu as pltpu
from jax.sharding import Mesh, PartitionSpec as P


def exchange_sum(value, axis):
    size = lax.axis_size(axis)
    stride = 1
    while stride < size:
        pairs = [(i, i ^ stride) for i in range(size)]
        value = value + lax.ppermute(value, axis, pairs)
        stride *= 2
    return value


def split_pair(x):
    scaled = x * 65537.0
    hi = scaled - (scaled - x)
    lo = x - hi
    return hi.astype(jnp.bfloat16), lo.astype(jnp.bfloat16)


def gram_of(x):
    hi, lo = split_pair(x)
    both = jnp.concatenate([hi, lo], axis=1)
    full = lax.dot_general(
        both, both, (((0,), (0,)), ((), ())), preferred_element_type=jnp.float32
    )
    n = x.shape[1]
    return (full[:n, :n] + full[n:, n:]) + (full[:n, n:] + full[n:, :n])


def project_kernel(t_ref, b_ref, o_ref):
    rank_cols = o_ref.shape[1]
    hi, lo = split_pair(t_ref[...])
    pair = b_ref[...]
    acc = jnp.dot(hi, pair, preferred_element_type=jnp.float32)
    acc = acc + jnp.dot(lo, pair, preferred_element_type=jnp.float32)
    o_ref[...] = acc[:, :rank_cols] + acc[:, rank_cols:]


def project(flat, bin_factor, first_row, rows, block_rows=4096):
    bin_count = flat.shape[1]
    start = first_row // block_rows
    rank_cols = bin_factor.shape[1]
    b_hi, b_lo = split_pair(bin_factor)
    pair = jnp.concatenate([b_hi, b_lo], axis=1)
    return pl.pallas_call(
        project_kernel,
        out_shape=jax.ShapeDtypeStruct((rows, rank_cols), jnp.float32),
        grid=(rows // block_rows,),
        in_specs=[
            pl.BlockSpec((block_rows, bin_count), lambda i: (i + start, 0)),
            pl.BlockSpec((bin_count, 2 * rank_cols), lambda i: (0, 0)),
        ],
        out_specs=pl.BlockSpec((block_rows, rank_cols), lambda i: (i, 0)),
        cost_estimate=pl.CostEstimate(
            flops=8 * rows * bin_count * rank_cols,
            transcendentals=0,
            bytes_accessed=4 * rows * (bin_count + rank_cols),
        ),
    )(flat, pair)


def gather_cells(cell_factor, project_first):
    outer = lax.axis_size("cell_outer")
    spread = jnp.broadcast_to(cell_factor[None], (outer,) + cell_factor.shape)
    mine = lax.all_to_all(spread, "cell_outer", 0, 0, tiled=True)
    mine, first_part = lax.optimization_barrier((mine, project_first()))
    core_count = lax.axis_size("cell_core")
    if core_count == 1:
        return mine.reshape(-1, cell_factor.shape[1]), first_part
    other = lax.ppermute(mine, "cell_core", [(0, 1), (1, 0)])
    first = lax.axis_index("cell_core") == 0
    pair = (jnp.where(first, mine, other), jnp.where(first, other, mine))
    return jnp.stack(pair, axis=1).reshape(-1, cell_factor.shape[1]), first_part


def body(tensor, cell_factor, bin_factor):
    image_rows, cell_count, bin_count = tensor.shape
    rank_cols = bin_factor.shape[1]
    rows = image_rows * cell_count
    flat = tensor.reshape(rows, bin_count)
    gram_bin = exchange_sum(gram_of(bin_factor), "bin")
    cell_full, projected = gather_cells(
        cell_factor, lambda: project(flat, bin_factor, 0, rows)
    )
    projected = projected.reshape(image_rows, cell_count, rank_cols)
    mttkrp = jnp.sum(projected * cell_full[None], axis=1)
    gram = gram_of(cell_full) * gram_bin
    chol_lower = jnp.linalg.cholesky(gram)
    totals = exchange_sum(mttkrp, "bin")
    solved = jax.scipy.linalg.cho_solve((chol_lower, True), totals.T).T
    own_cols = rank_cols // lax.axis_size("bin")
    updated = lax.dynamic_slice_in_dim(solved, lax.axis_index("bin") * own_cols, own_cols, 1)
    return updated


def solution(mesh):
    cell_size, bin_size = mesh.shape["cell"], mesh.shape["bin"]
    core_count = 2 if cell_size % 2 == 0 else 1
    split = Mesh(
        mesh.devices.reshape(cell_size // core_count, core_count, bin_size),
        ("cell_outer", "cell_core", "bin"),
    )
    cell = ("cell_outer", "cell_core")
    placed = (P(cell, None, "bin"), P(cell, None), P("bin", None))
    return jax.shard_map(
        body, mesh=split, in_specs=placed, out_specs=P(cell, "bin"), check_vma=False
    )
```

```python
import jax
import jax.numpy as jnp
from jax import lax
from jax.experimental import pallas as pl
from jax.experimental.pallas import tpu as pltpu
from jax.sharding import Mesh, PartitionSpec as P


def exchange_sum(value, axis):
    size = lax.axis_size(axis)
    stride = 1
    while stride < size:
        pairs = [(i, i ^ stride) for i in range(size)]
        value = value + lax.ppermute(value, axis, pairs)
        stride *= 2
    return value


def split_pair(x):
    scaled = x * 65537.0
    hi = scaled - (scaled - x)
    lo = x - hi
    return hi.astype(jnp.bfloat16), lo.astype(jnp.bfloat16)


def gram_of(x):
    hi, lo = split_pair(x)
    both = jnp.concatenate([hi, lo], axis=1)
    full = lax.dot_general(
        both, both, (((0,), (0,)), ((), ())), preferred_element_type=jnp.float32
    )
    n = x.shape[1]
    return (full[:n, :n] + full[n:, n:]) + (full[:n, n:] + full[n:, :n])


def project_kernel(t_ref, b_ref, o_ref):
    rank_cols = o_ref.shape[1]
    hi, lo = split_pair(t_ref[...])
    pair = b_ref[...]
    acc = jnp.dot(hi, pair, preferred_element_type=jnp.float32)
    acc = acc + jnp.dot(lo, pair, preferred_element_type=jnp.float32)
    o_ref[...] = acc[:, :rank_cols] + acc[:, rank_cols:]


def project(flat, bin_factor, first_row, rows, block_rows=4096):
    bin_count = flat.shape[1]
    start = first_row // block_rows
    rank_cols = bin_factor.shape[1]
    b_hi, b_lo = split_pair(bin_factor)
    pair = jnp.concatenate([b_hi, b_lo], axis=1)
    return pl.pallas_call(
        project_kernel,
        out_shape=jax.ShapeDtypeStruct((rows, rank_cols), jnp.float32),
        grid=(rows // block_rows,),
        in_specs=[
            pl.BlockSpec((block_rows, bin_count), lambda i: (i + start, 0)),
            pl.BlockSpec((bin_count, 2 * rank_cols), lambda i: (0, 0)),
        ],
        out_specs=pl.BlockSpec((block_rows, rank_cols), lambda i: (i, 0)),
        cost_estimate=pl.CostEstimate(
            flops=8 * rows * bin_count * rank_cols,
            transcendentals=0,
            bytes_accessed=4 * rows * (bin_count + rank_cols),
        ),
    )(flat, pair)


def gather_cells(cell_factor, project_first):
    outer = lax.axis_size("cell_outer")
    spread = jnp.broadcast_to(cell_factor[None], (outer,) + cell_factor.shape)
    mine = lax.all_to_all(spread, "cell_outer", 0, 0, tiled=True)
    mine, first_part = lax.optimization_barrier((mine, project_first()))
    core_count = lax.axis_size("cell_core")
    if core_count == 1:
        return mine.reshape(-1, cell_factor.shape[1]), first_part
    other = lax.ppermute(mine, "cell_core", [(0, 1), (1, 0)])
    first = lax.axis_index("cell_core") == 0
    pair = (jnp.where(first, mine, other), jnp.where(first, other, mine))
    return jnp.stack(pair, axis=1).reshape(-1, cell_factor.shape[1]), first_part


def sweep_kernel(g_ref, o_ref):
    n = g_ref.shape[0]
    sub = lax.broadcasted_iota(jnp.int32, (n, n), 0)
    lane = lax.broadcasted_iota(jnp.int32, (n, n), 1)

    def step(k, a):
        on_row = sub == k
        on_col = lane == k
        row = jnp.sum(jnp.where(on_row, a, 0.0), axis=0, keepdims=True)
        col = jnp.sum(jnp.where(on_col, a, 0.0), axis=1, keepdims=True)
        pivot = jnp.sum(jnp.where(on_col[:1], row, 0.0), axis=1, keepdims=True)
        inv = 1.0 / pivot
        scaled_row = row * inv
        upd = a - col * scaled_row
        upd = jnp.where(on_col, col * inv, upd)
        upd = jnp.where(on_row, scaled_row, upd)
        return jnp.where(on_row & on_col, -inv, upd)

    o_ref[...] = lax.fori_loop(0, n, step, g_ref[...], unroll=8)


def negated_inverse(gram):
    return pl.pallas_call(
        sweep_kernel, out_shape=jax.ShapeDtypeStruct(gram.shape, jnp.float32)
    )(gram)


def body(tensor, cell_factor, bin_factor):
    image_rows, cell_count, bin_count = tensor.shape
    rank_cols = bin_factor.shape[1]
    rows = image_rows * cell_count
    flat = tensor.reshape(rows, bin_count)
    gram_bin = exchange_sum(gram_of(bin_factor), "bin")
    cell_full, projected = gather_cells(
        cell_factor, lambda: project(flat, bin_factor, 0, rows)
    )
    projected = projected.reshape(image_rows, cell_count, rank_cols)
    mttkrp = jnp.sum(projected * cell_full[None], axis=1)
    gram = gram_of(cell_full) * gram_bin
    neg_inv = negated_inverse(gram)
    totals = exchange_sum(mttkrp, "bin")
    own_cols = rank_cols // lax.axis_size("bin")
    own = lax.dynamic_slice_in_dim(neg_inv, lax.axis_index("bin") * own_cols, own_cols, 1)
    return -jnp.dot(totals, own, precision=lax.Precision.HIGHEST)


def solution(mesh):
    cell_size, bin_size = mesh.shape["cell"], mesh.shape["bin"]
    core_count = 2 if cell_size % 2 == 0 else 1
    split = Mesh(
        mesh.devices.reshape(cell_size // core_count, core_count, bin_size),
        ("cell_outer", "cell_core", "bin"),
    )
    cell = ("cell_outer", "cell_core")
    placed = (P(cell, None, "bin"), P(cell, None), P("bin", None))
    return jax.shard_map(
        body, mesh=split, in_specs=placed, out_specs=P(cell, "bin"), check_vma=False
    )
```

```python
import jax
import jax.numpy as jnp
from jax import lax
from jax.experimental import pallas as pl
from jax.experimental.pallas import tpu as pltpu
from jax.sharding import Mesh, PartitionSpec as P


def exchange_sum(value, axis):
    size = lax.axis_size(axis)
    stride = 1
    while stride < size:
        pairs = [(i, i ^ stride) for i in range(size)]
        value = value + lax.ppermute(value, axis, pairs)
        stride *= 2
    return value


def split_pair(x):
    scaled = x * 65537.0
    hi = scaled - (scaled - x)
    lo = x - hi
    return hi.astype(jnp.bfloat16), lo.astype(jnp.bfloat16)


def gram_of(x):
    hi, lo = split_pair(x)
    both = jnp.concatenate([hi, lo], axis=1)
    full = lax.dot_general(
        both, both, (((0,), (0,)), ((), ())), preferred_element_type=jnp.float32
    )
    n = x.shape[1]
    return (full[:n, :n] + full[n:, n:]) + (full[:n, n:] + full[n:, :n])


def project_kernel(t_ref, b_ref, o_ref):
    rank_cols = o_ref.shape[1]
    hi, lo = split_pair(t_ref[...])
    pair = b_ref[...]
    acc = jnp.dot(hi, pair, preferred_element_type=jnp.float32)
    acc = acc + jnp.dot(lo, pair, preferred_element_type=jnp.float32)
    o_ref[...] = acc[:, :rank_cols] + acc[:, rank_cols:]


def project(flat, bin_factor, first_row, rows, block_rows=4096):
    bin_count = flat.shape[1]
    start = first_row // block_rows
    rank_cols = bin_factor.shape[1]
    b_hi, b_lo = split_pair(bin_factor)
    pair = jnp.concatenate([b_hi, b_lo], axis=1)
    return pl.pallas_call(
        project_kernel,
        out_shape=jax.ShapeDtypeStruct((rows, rank_cols), jnp.float32),
        grid=(rows // block_rows,),
        in_specs=[
            pl.BlockSpec((block_rows, bin_count), lambda i: (i + start, 0)),
            pl.BlockSpec((bin_count, 2 * rank_cols), lambda i: (0, 0)),
        ],
        out_specs=pl.BlockSpec((block_rows, rank_cols), lambda i: (i, 0)),
        cost_estimate=pl.CostEstimate(
            flops=8 * rows * bin_count * rank_cols,
            transcendentals=0,
            bytes_accessed=4 * rows * (bin_count + rank_cols),
        ),
    )(flat, pair)


def gather_cells(cell_factor, project_all):
    outer = lax.axis_size("cell_outer")
    spread = jnp.broadcast_to(cell_factor[None], (outer,) + cell_factor.shape)
    mine = lax.all_to_all(spread, "cell_outer", 0, 0, tiled=True)
    mine, projected = lax.optimization_barrier((mine, project_all()))
    core_count = lax.axis_size("cell_core")
    if core_count == 1:
        return [mine], projected
    other = lax.ppermute(mine, "cell_core", [(0, 1), (1, 0)])
    first = lax.axis_index("cell_core") == 0
    return [jnp.where(first, mine, other), jnp.where(first, other, mine)], projected


def sweep_kernel(g_ref, o_ref):
    n = g_ref.shape[0]
    sub = lax.broadcasted_iota(jnp.int32, (n, n), 0)
    lane = lax.broadcasted_iota(jnp.int32, (n, n), 1)

    def step(k, a):
        on_row = sub == k
        on_col = lane == k
        row = jnp.sum(jnp.where(on_row, a, 0.0), axis=0, keepdims=True)
        col = jnp.sum(jnp.where(on_col, a, 0.0), axis=1, keepdims=True)
        pivot = jnp.sum(jnp.where(on_col[:1], row, 0.0), axis=1, keepdims=True)
        inv = 1.0 / pivot
        scaled_row = row * inv
        upd = a - col * scaled_row
        upd = jnp.where(on_col, col * inv, upd)
        upd = jnp.where(on_row, scaled_row, upd)
        return jnp.where(on_row & on_col, -inv, upd)

    o_ref[...] = lax.fori_loop(0, n, step, g_ref[...], unroll=8)


def negated_inverse(gram):
    return pl.pallas_call(
        sweep_kernel, out_shape=jax.ShapeDtypeStruct(gram.shape, jnp.float32)
    )(gram)


def body(tensor, cell_factor, bin_factor):
    image_rows, cell_count, bin_count = tensor.shape
    rank_cols = bin_factor.shape[1]
    rows = image_rows * cell_count
    flat = tensor.reshape(rows, bin_count)
    gram_bin = exchange_sum(gram_of(bin_factor), "bin")
    blocks, projected = gather_cells(
        cell_factor, lambda: project(flat, bin_factor, 0, rows)
    )
    outer, block_rows = blocks[0].shape[:2]
    projected = projected.reshape(image_rows, outer, len(blocks), block_rows, rank_cols)
    mttkrp = sum(
        jnp.sum(projected[:, :, c] * blocks[c][None], axis=(1, 2)) for c in range(len(blocks))
    )
    gram_cell = sum(gram_of(b.reshape(-1, rank_cols)) for b in blocks)
    gram = gram_cell * gram_bin
    neg_inv = negated_inverse(gram)
    totals = exchange_sum(mttkrp, "bin")
    own_cols = rank_cols // lax.axis_size("bin")
    own = lax.dynamic_slice_in_dim(neg_inv, lax.axis_index("bin") * own_cols, own_cols, 1)
    return -jnp.dot(totals, own, precision=lax.Precision.HIGHEST)


def solution(mesh):
    cell_size, bin_size = mesh.shape["cell"], mesh.shape["bin"]
    core_count = 2 if cell_size % 2 == 0 else 1
    split = Mesh(
        mesh.devices.reshape(cell_size // core_count, core_count, bin_size),
        ("cell_outer", "cell_core", "bin"),
    )
    cell = ("cell_outer", "cell_core")
    placed = (P(cell, None, "bin"), P(cell, None), P("bin", None))
    return jax.shard_map(
        body, mesh=split, in_specs=placed, out_specs=P(cell, "bin"), check_vma=False
    )
```

```python
import jax
import jax.numpy as jnp
from jax import lax
from jax.experimental import pallas as pl
from jax.experimental.pallas import tpu as pltpu
from jax.sharding import Mesh, PartitionSpec as P


def exchange_sum(value, axis):
    size = lax.axis_size(axis)
    stride = 1
    while stride < size:
        pairs = [(i, i ^ stride) for i in range(size)]
        value = value + lax.ppermute(value, axis, pairs)
        stride *= 2
    return value


def split_pair(x):
    scaled = x * 65537.0
    hi = scaled - (scaled - x)
    lo = x - hi
    return hi.astype(jnp.bfloat16), lo.astype(jnp.bfloat16)


def gram_of(x):
    hi, lo = split_pair(x)
    both = jnp.concatenate([hi, lo], axis=1)
    full = lax.dot_general(
        both, both, (((0,), (0,)), ((), ())), preferred_element_type=jnp.float32
    )
    n = x.shape[1]
    return (full[:n, :n] + full[n:, n:]) + (full[:n, n:] + full[n:, :n])


def project_kernel(t_ref, b_ref, o_ref):
    rank_cols = o_ref.shape[1]
    hi, lo = split_pair(t_ref[...])
    pair = b_ref[...]
    acc = jnp.dot(hi, pair, preferred_element_type=jnp.float32)
    acc = acc + jnp.dot(lo, pair, preferred_element_type=jnp.float32)
    o_ref[...] = acc[:, :rank_cols] + acc[:, rank_cols:]


def project(flat, bin_factor, first_row, rows, block_rows=4096):
    bin_count = flat.shape[1]
    start = first_row // block_rows
    rank_cols = bin_factor.shape[1]
    b_hi, b_lo = split_pair(bin_factor)
    pair = jnp.concatenate([b_hi, b_lo], axis=1)
    return pl.pallas_call(
        project_kernel,
        out_shape=jax.ShapeDtypeStruct((rows, rank_cols), jnp.float32),
        grid=(rows // block_rows,),
        in_specs=[
            pl.BlockSpec((block_rows, bin_count), lambda i: (i + start, 0)),
            pl.BlockSpec((bin_count, 2 * rank_cols), lambda i: (0, 0)),
        ],
        out_specs=pl.BlockSpec((block_rows, rank_cols), lambda i: (i, 0)),
        cost_estimate=pl.CostEstimate(
            flops=8 * rows * bin_count * rank_cols,
            transcendentals=0,
            bytes_accessed=4 * rows * (bin_count + rank_cols),
        ),
    )(flat, pair)


def gather_cells(cell_factor, early_work):
    outer = lax.axis_size("cell_outer")
    spread = jnp.broadcast_to(cell_factor[None], (outer,) + cell_factor.shape)
    mine = lax.all_to_all(spread, "cell_outer", 0, 0, tiled=True)
    mine, early = lax.optimization_barrier((mine, early_work()))
    core_count = lax.axis_size("cell_core")
    if core_count == 1:
        return [mine], early
    other = lax.ppermute(mine, "cell_core", [(0, 1), (1, 0)])
    first = lax.axis_index("cell_core") == 0
    return [jnp.where(first, mine, other), jnp.where(first, other, mine)], early


def sweep_kernel(g_ref, o_ref):
    n = g_ref.shape[0]
    sub = lax.broadcasted_iota(jnp.int32, (n, n), 0)
    lane = lax.broadcasted_iota(jnp.int32, (n, n), 1)

    def step(k, a):
        on_row = sub == k
        on_col = lane == k
        row = jnp.sum(jnp.where(on_row, a, 0.0), axis=0, keepdims=True)
        col = jnp.sum(jnp.where(on_col, a, 0.0), axis=1, keepdims=True)
        pivot = jnp.sum(jnp.where(on_col[:1], row, 0.0), axis=1, keepdims=True)
        inv = 1.0 / pivot
        scaled_row = row * inv
        upd = a - col * scaled_row
        upd = jnp.where(on_col, col * inv, upd)
        upd = jnp.where(on_row, scaled_row, upd)
        return jnp.where(on_row & on_col, -inv, upd)

    o_ref[...] = lax.fori_loop(0, n, step, g_ref[...], unroll=8)


def negated_inverse(gram):
    return pl.pallas_call(
        sweep_kernel, out_shape=jax.ShapeDtypeStruct(gram.shape, jnp.float32)
    )(gram)


def body(tensor, cell_factor, bin_factor):
    image_rows, cell_count, bin_count = tensor.shape
    rank_cols = bin_factor.shape[1]
    rows = image_rows * cell_count
    flat = tensor.reshape(rows, bin_count)
    blocks, (projected, gram_bin) = gather_cells(
        cell_factor,
        lambda: (project(flat, bin_factor, 0, rows), exchange_sum(gram_of(bin_factor), "bin")),
    )
    outer, block_rows = blocks[0].shape[:2]
    projected = projected.reshape(image_rows, outer, len(blocks), block_rows, rank_cols)
    mttkrp = sum(
        jnp.sum(projected[:, :, c] * blocks[c][None], axis=(1, 2)) for c in range(len(blocks))
    )
    gram_cell = sum(gram_of(b.reshape(-1, rank_cols)) for b in blocks)
    gram = gram_cell * gram_bin
    neg_inv = negated_inverse(gram)
    totals = exchange_sum(mttkrp, "bin")
    own_cols = rank_cols // lax.axis_size("bin")
    own = lax.dynamic_slice_in_dim(neg_inv, lax.axis_index("bin") * own_cols, own_cols, 1)
    return -jnp.dot(totals, own, precision=lax.Precision.HIGHEST)


def solution(mesh):
    cell_size, bin_size = mesh.shape["cell"], mesh.shape["bin"]
    core_count = 2 if cell_size % 2 == 0 else 1
    split = Mesh(
        mesh.devices.reshape(cell_size // core_count, core_count, bin_size),
        ("cell_outer", "cell_core", "bin"),
    )
    cell = ("cell_outer", "cell_core")
    placed = (P(cell, None, "bin"), P(cell, None), P("bin", None))
    return jax.shard_map(
        body, mesh=split, in_specs=placed, out_specs=P(cell, "bin"), check_vma=False
    )
```

```python
import jax
import jax.numpy as jnp
from jax import lax
from jax.experimental import pallas as pl
from jax.experimental.pallas import tpu as pltpu
from jax.sharding import Mesh, PartitionSpec as P


def exchange_sum(value, axis):
    size = lax.axis_size(axis)
    stride = 1
    while stride < size:
        pairs = [(i, i ^ stride) for i in range(size)]
        value = value + lax.ppermute(value, axis, pairs)
        stride *= 2
    return value


def split_pair(x):
    scaled = x * 65537.0
    hi = scaled - (scaled - x)
    lo = x - hi
    return hi.astype(jnp.bfloat16), lo.astype(jnp.bfloat16)


def gram_of(x):
    hi, lo = split_pair(x)
    both = jnp.concatenate([hi, lo], axis=1)
    full = lax.dot_general(
        both, both, (((0,), (0,)), ((), ())), preferred_element_type=jnp.float32
    )
    n = x.shape[1]
    return (full[:n, :n] + full[n:, n:]) + (full[:n, n:] + full[n:, :n])


def project_kernel(t_ref, b_ref, o_ref):
    rank_cols = o_ref.shape[1]
    hi, lo = split_pair(t_ref[...])
    pair = b_ref[...]
    acc = jnp.dot(hi, pair, preferred_element_type=jnp.float32)
    acc = acc + jnp.dot(lo, pair, preferred_element_type=jnp.float32)
    o_ref[...] = acc[:, :rank_cols] + acc[:, rank_cols:]


def project(flat, bin_factor, first_row, rows, block_rows=4096):
    bin_count = flat.shape[1]
    start = first_row // block_rows
    rank_cols = bin_factor.shape[1]
    b_hi, b_lo = split_pair(bin_factor)
    pair = jnp.concatenate([b_hi, b_lo], axis=1)
    return pl.pallas_call(
        project_kernel,
        out_shape=jax.ShapeDtypeStruct((rows, rank_cols), jnp.float32),
        grid=(rows // block_rows,),
        in_specs=[
            pl.BlockSpec((block_rows, bin_count), lambda i: (i + start, 0)),
            pl.BlockSpec((bin_count, 2 * rank_cols), lambda i: (0, 0)),
        ],
        out_specs=pl.BlockSpec((block_rows, rank_cols), lambda i: (i, 0)),
        cost_estimate=pl.CostEstimate(
            flops=8 * rows * bin_count * rank_cols,
            transcendentals=0,
            bytes_accessed=4 * rows * (bin_count + rank_cols),
        ),
    )(flat, pair)


def gather_cells(cell_factor, project_all):
    outer = lax.axis_size("cell_outer")
    spread = jnp.broadcast_to(cell_factor[None], (outer,) + cell_factor.shape)
    mine = lax.all_to_all(spread, "cell_outer", 0, 0, tiled=True)
    mine, projected = lax.optimization_barrier((mine, project_all()))
    core_count = lax.axis_size("cell_core")
    if core_count == 1:
        return [mine], projected
    other = lax.ppermute(mine, "cell_core", [(0, 1), (1, 0)])
    first = lax.axis_index("cell_core") == 0
    return [jnp.where(first, mine, other), jnp.where(first, other, mine)], projected


def sweep_kernel(g_ref, o_ref):
    n = g_ref.shape[0]
    sub = lax.broadcasted_iota(jnp.int32, (n, n), 0)
    lane = lax.broadcasted_iota(jnp.int32, (n, n), 1)

    def step(k, a):
        on_row = sub == k
        on_col = lane == k
        row = jnp.sum(jnp.where(on_row, a, 0.0), axis=0, keepdims=True)
        col = jnp.sum(jnp.where(on_col, a, 0.0), axis=1, keepdims=True)
        pivot = jnp.sum(jnp.where(on_col[:1], row, 0.0), axis=1, keepdims=True)
        inv = 1.0 / pivot
        scaled_row = row * inv
        upd = a - col * scaled_row
        upd = jnp.where(on_col, col * inv, upd)
        upd = jnp.where(on_row, scaled_row, upd)
        return jnp.where(on_row & on_col, -inv, upd)

    o_ref[...] = lax.fori_loop(0, n, step, g_ref[...], unroll=8)


def negated_inverse(gram):
    return pl.pallas_call(
        sweep_kernel, out_shape=jax.ShapeDtypeStruct(gram.shape, jnp.float32)
    )(gram)


def fused_kernel(g_ref, p_ref, x0_ref, x1_ref, o_ref, m_ref, a_ref):
    o = pl.program_id(0)
    n = g_ref.shape[0]
    share = n // pl.num_programs(0)
    sub = lax.broadcasted_iota(jnp.int32, (n, n), 0)
    lane = lax.broadcasted_iota(jnp.int32, (n, n), 1)

    @pl.when(o == 0)
    def _():
        a_ref[...] = g_ref[...]
        m_ref[...] = jnp.zeros_like(m_ref)

    def step(s, a):
        k = o * share + s
        on_row = sub == k
        on_col = lane == k
        row = jnp.sum(jnp.where(on_row, a, 0.0), axis=0, keepdims=True)
        col = jnp.sum(jnp.where(on_col, a, 0.0), axis=1, keepdims=True)
        pivot = jnp.sum(jnp.where(on_col[:1], row, 0.0), axis=1, keepdims=True)
        inv = 1.0 / pivot
        scaled_row = row * inv
        upd = a - col * scaled_row
        upd = jnp.where(on_col, col * inv, upd)
        upd = jnp.where(on_row, scaled_row, upd)
        return jnp.where(on_row & on_col, -inv, upd)

    a_ref[...] = lax.fori_loop(0, share, step, a_ref[...], unroll=8)
    p = p_ref[...]
    m_ref[...] += jnp.sum(p[:, 0, 0] * x0_ref[...], axis=1) + jnp.sum(
        p[:, 0, 1] * x1_ref[...], axis=1
    )
    o_ref[...] = a_ref[...]


def fused_solve_parts(gram, projected, x0, x1):
    images, outer, _, rows, rank = projected.shape
    n = gram.shape[0]
    return pl.pallas_call(
        fused_kernel,
        out_shape=(
            jax.ShapeDtypeStruct(gram.shape, jnp.float32),
            jax.ShapeDtypeStruct((images, rank), jnp.float32),
        ),
        grid=(outer,),
        in_specs=[
            pl.BlockSpec((n, n), lambda o: (0, 0)),
            pl.BlockSpec((images, 1, 2, rows, rank), lambda o: (0, o, 0, 0, 0)),
            pl.BlockSpec((1, rows, rank), lambda o: (o, 0, 0)),
            pl.BlockSpec((1, rows, rank), lambda o: (o, 0, 0)),
        ],
        out_specs=(
            pl.BlockSpec((n, n), lambda o: (0, 0)),
            pl.BlockSpec((images, rank), lambda o: (0, 0)),
        ),
        scratch_shapes=[pltpu.VMEM((n, n), jnp.float32)],
    )(gram, projected, x0, x1)


def body(tensor, cell_factor, bin_factor):
    image_rows, cell_count, bin_count = tensor.shape
    rank_cols = bin_factor.shape[1]
    rows = image_rows * cell_count
    flat = tensor.reshape(rows, bin_count)
    gram_bin = exchange_sum(gram_of(bin_factor), "bin")
    blocks, projected = gather_cells(
        cell_factor, lambda: project(flat, bin_factor, 0, rows)
    )
    outer, block_rows = blocks[0].shape[:2]
    projected = projected.reshape(image_rows, outer, len(blocks), block_rows, rank_cols)
    gram_cell = sum(gram_of(b.reshape(-1, rank_cols)) for b in blocks)
    gram = gram_cell * gram_bin
    if len(blocks) == 2 and rank_cols % outer == 0:
        neg_inv, mttkrp = fused_solve_parts(gram, projected, blocks[0], blocks[1])
    else:
        mttkrp = sum(
            jnp.sum(projected[:, :, c] * blocks[c][None], axis=(1, 2))
            for c in range(len(blocks))
        )
        neg_inv = negated_inverse(gram)
    totals = exchange_sum(mttkrp, "bin")
    own_cols = rank_cols // lax.axis_size("bin")
    own = lax.dynamic_slice_in_dim(neg_inv, lax.axis_index("bin") * own_cols, own_cols, 1)
    return -jnp.dot(totals, own, precision=lax.Precision.HIGHEST)


def solution(mesh):
    cell_size, bin_size = mesh.shape["cell"], mesh.shape["bin"]
    core_count = 2 if cell_size % 2 == 0 else 1
    split = Mesh(
        mesh.devices.reshape(cell_size // core_count, core_count, bin_size),
        ("cell_outer", "cell_core", "bin"),
    )
    cell = ("cell_outer", "cell_core")
    placed = (P(cell, None, "bin"), P(cell, None), P("bin", None))
    return jax.shard_map(
        body, mesh=split, in_specs=placed, out_specs=P(cell, "bin"), check_vma=False
    )
```

```python
import functools

import jax
import jax.numpy as jnp
from jax import lax
from jax.experimental import pallas as pl
from jax.experimental.pallas import tpu as pltpu
from jax.sharding import Mesh, PartitionSpec as P


def exchange_sum(value, axis):
    size = lax.axis_size(axis)
    stride = 1
    while stride < size:
        pairs = [(i, i ^ stride) for i in range(size)]
        value = value + lax.ppermute(value, axis, pairs)
        stride *= 2
    return value


def split_pair(x):
    scaled = x * 65537.0
    hi = scaled - (scaled - x)
    lo = x - hi
    return hi.astype(jnp.bfloat16), lo.astype(jnp.bfloat16)


def gram_of(x):
    hi, lo = split_pair(x)
    both = jnp.concatenate([hi, lo], axis=1)
    full = lax.dot_general(
        both, both, (((0,), (0,)), ((), ())), preferred_element_type=jnp.float32
    )
    n = x.shape[1]
    return (full[:n, :n] + full[n:, n:]) + (full[:n, n:] + full[n:, :n])


def project_kernel(t_ref, b_ref, o_ref):
    rank_cols = o_ref.shape[1]
    hi, lo = split_pair(t_ref[...])
    pair = b_ref[...]
    acc = jnp.dot(hi, pair, preferred_element_type=jnp.float32)
    acc = acc + jnp.dot(lo, pair, preferred_element_type=jnp.float32)
    o_ref[...] = acc[:, :rank_cols] + acc[:, rank_cols:]


def project(flat, bin_factor, first_row, rows, block_rows=4096):
    bin_count = flat.shape[1]
    start = first_row // block_rows
    rank_cols = bin_factor.shape[1]
    b_hi, b_lo = split_pair(bin_factor)
    pair = jnp.concatenate([b_hi, b_lo], axis=1)
    return pl.pallas_call(
        project_kernel,
        out_shape=jax.ShapeDtypeStruct((rows, rank_cols), jnp.float32),
        grid=(rows // block_rows,),
        in_specs=[
            pl.BlockSpec((block_rows, bin_count), lambda i: (i + start, 0)),
            pl.BlockSpec((bin_count, 2 * rank_cols), lambda i: (0, 0)),
        ],
        out_specs=pl.BlockSpec((block_rows, rank_cols), lambda i: (i, 0)),
        cost_estimate=pl.CostEstimate(
            flops=8 * rows * bin_count * rank_cols,
            transcendentals=0,
            bytes_accessed=4 * rows * (bin_count + rank_cols),
        ),
    )(flat, pair)


def gather_cells(cell_factor, early_work):
    outer = lax.axis_size("cell_outer")
    spread = jnp.broadcast_to(cell_factor[None], (outer,) + cell_factor.shape)
    mine = lax.all_to_all(spread, "cell_outer", 0, 0, tiled=True)
    mine, early = lax.optimization_barrier((mine, early_work()))
    if lax.axis_size("cell_core") == 1:
        return mine, None, early
    other = lax.ppermute(mine, "cell_core", [(0, 1), (1, 0)])
    return mine, other, early


def sweep_steps(a, first, count):
    n = a.shape[0]
    sub = lax.broadcasted_iota(jnp.int32, (n, n), 0)
    lane = lax.broadcasted_iota(jnp.int32, (n, n), 1)

    def step(s, a):
        k = first + s
        on_row = sub == k
        on_col = lane == k
        row = jnp.sum(jnp.where(on_row, a, 0.0), axis=0, keepdims=True)
        col = jnp.sum(jnp.where(on_col, a, 0.0), axis=1, keepdims=True)
        pivot = jnp.sum(jnp.where(on_col[:1], row, 0.0), axis=1, keepdims=True)
        inv = 1.0 / pivot
        scaled_row = row * inv
        upd = a - col * scaled_row
        upd = jnp.where(on_col, col * inv, upd)
        upd = jnp.where(on_row, scaled_row, upd)
        return jnp.where(on_row & on_col, -inv, upd)

    return lax.fori_loop(0, count, step, a, unroll=8)


def sweep_kernel(first, g_ref, o_ref):
    o_ref[...] = sweep_steps(g_ref[...], first, g_ref.shape[0] - first)


def sweep_rest(a, first):
    return pl.pallas_call(
        functools.partial(sweep_kernel, first),
        out_shape=jax.ShapeDtypeStruct(a.shape, jnp.float32),
    )(a)


def fused_kernel(core_ref, g_ref, pm_ref, po_ref, xm_ref, xo_ref, o_ref, m_ref, a_ref):
    o = pl.program_id(0)
    share = g_ref.shape[0] // (2 * pl.num_programs(0))

    @pl.when(o == 0)
    def _():
        a_ref[...] = g_ref[...]
        m_ref[...] = jnp.zeros_like(m_ref)

    a_ref[...] = sweep_steps(a_ref[...], o * share, share)
    m_ref[...] += jnp.sum(pm_ref[:, 0, 0] * xm_ref[...], axis=1) + jnp.sum(
        po_ref[:, 0, 0] * xo_ref[...], axis=1
    )
    o_ref[...] = a_ref[...]


def fused_half(gram, projected, mine, other, core):
    images, outer, _, rows, rank = projected.shape
    n = gram.shape[0]
    p_block = (images, 1, 1, rows, rank)
    grid_spec = pltpu.PrefetchScalarGridSpec(
        num_scalar_prefetch=1,
        grid=(outer,),
        in_specs=[
            pl.BlockSpec((n, n), lambda o, c: (0, 0)),
            pl.BlockSpec(p_block, lambda o, c: (0, o, c[0], 0, 0)),
            pl.BlockSpec(p_block, lambda o, c: (0, o, 1 - c[0], 0, 0)),
            pl.BlockSpec((1, rows, rank), lambda o, c: (o, 0, 0)),
            pl.BlockSpec((1, rows, rank), lambda o, c: (o, 0, 0)),
        ],
        out_specs=(
            pl.BlockSpec((n, n), lambda o, c: (0, 0)),
            pl.BlockSpec((images, rank), lambda o, c: (0, 0)),
        ),
        scratch_shapes=[pltpu.VMEM((n, n), jnp.float32)],
    )
    return pl.pallas_call(
        fused_kernel,
        out_shape=(
            jax.ShapeDtypeStruct(gram.shape, jnp.float32),
            jax.ShapeDtypeStruct((images, rank), jnp.float32),
        ),
        grid_spec=grid_spec,
    )(core, gram, projected, projected, mine, other)


def body(tensor, cell_factor, bin_factor):
    image_rows, cell_count, bin_count = tensor.shape
    rank_cols = bin_factor.shape[1]
    rows = image_rows * cell_count
    flat = tensor.reshape(rows, bin_count)
    gram_bin = exchange_sum(gram_of(bin_factor), "bin")
    mine, other, projected = gather_cells(
        cell_factor, lambda: project(flat, bin_factor, 0, rows)
    )
    outer, block_rows = mine.shape[:2]
    blocks = [mine] if other is None else [mine, other]
    gram_cell = sum(gram_of(b.reshape(-1, rank_cols)) for b in blocks)
    gram = gram_cell * gram_bin
    half = rank_cols // 2
    projected = projected.reshape(image_rows, outer, len(blocks), block_rows, rank_cols)
    if other is not None and half % outer == 0:
        core = lax.axis_index("cell_core").astype(jnp.int32).reshape(1)
        partial, mttkrp = fused_half(gram, projected, mine, other, core)
        neg_inv = sweep_rest(partial, half)
    else:
        if other is None:
            mttkrp = jnp.sum(projected[:, :, 0] * mine[None], axis=(1, 2))
        else:
            first = lax.axis_index("cell_core") == 0
            x0, x1 = jnp.where(first, mine, other), jnp.where(first, other, mine)
            mttkrp = jnp.sum(projected[:, :, 0] * x0[None], axis=(1, 2)) + jnp.sum(
                projected[:, :, 1] * x1[None], axis=(1, 2)
            )
        neg_inv = sweep_rest(gram, 0)
    totals = exchange_sum(mttkrp, "bin")
    own_cols = rank_cols // lax.axis_size("bin")
    own = lax.dynamic_slice_in_dim(neg_inv, lax.axis_index("bin") * own_cols, own_cols, 1)
    return -jnp.dot(totals, own, precision=lax.Precision.HIGHEST)


def solution(mesh):
    cell_size, bin_size = mesh.shape["cell"], mesh.shape["bin"]
    core_count = 2 if cell_size % 2 == 0 else 1
    split = Mesh(
        mesh.devices.reshape(cell_size // core_count, core_count, bin_size),
        ("cell_outer", "cell_core", "bin"),
    )
    cell = ("cell_outer", "cell_core")
    placed = (P(cell, None, "bin"), P(cell, None), P("bin", None))
    return jax.shard_map(
        body, mesh=split, in_specs=placed, out_specs=P(cell, "bin"), check_vma=False
    )
```

```python
import functools

import jax
import jax.numpy as jnp
from jax import lax
from jax.experimental import pallas as pl
from jax.experimental.pallas import tpu as pltpu
from jax.sharding import Mesh, PartitionSpec as P


def exchange_sum(value, axis):
    size = lax.axis_size(axis)
    stride = 1
    while stride < size:
        pairs = [(i, i ^ stride) for i in range(size)]
        value = value + lax.ppermute(value, axis, pairs)
        stride *= 2
    return value


def split_pair(x):
    scaled = x * 65537.0
    hi = scaled - (scaled - x)
    lo = x - hi
    return hi.astype(jnp.bfloat16), lo.astype(jnp.bfloat16)


def gram_of(x):
    hi, lo = split_pair(x)
    both = jnp.concatenate([hi, lo], axis=1)
    full = lax.dot_general(
        both, both, (((0,), (0,)), ((), ())), preferred_element_type=jnp.float32
    )
    n = x.shape[1]
    return (full[:n, :n] + full[n:, n:]) + (full[:n, n:] + full[n:, :n])


def project_kernel(t_ref, b_ref, o_ref):
    rank_cols = o_ref.shape[1]
    hi, lo = split_pair(t_ref[...])
    pair = b_ref[...]
    acc = jnp.dot(hi, pair, preferred_element_type=jnp.float32)
    acc = acc + jnp.dot(lo, pair, preferred_element_type=jnp.float32)
    o_ref[...] = acc[:, :rank_cols] + acc[:, rank_cols:]


def project(flat, bin_factor, first_row, rows, block_rows=4096):
    bin_count = flat.shape[1]
    start = first_row // block_rows
    rank_cols = bin_factor.shape[1]
    b_hi, b_lo = split_pair(bin_factor)
    pair = jnp.concatenate([b_hi, b_lo], axis=1)
    return pl.pallas_call(
        project_kernel,
        out_shape=jax.ShapeDtypeStruct((rows, rank_cols), jnp.float32),
        grid=(rows // block_rows,),
        in_specs=[
            pl.BlockSpec((block_rows, bin_count), lambda i: (i + start, 0)),
            pl.BlockSpec((bin_count, 2 * rank_cols), lambda i: (0, 0)),
        ],
        out_specs=pl.BlockSpec((block_rows, rank_cols), lambda i: (i, 0)),
        cost_estimate=pl.CostEstimate(
            flops=8 * rows * bin_count * rank_cols,
            transcendentals=0,
            bytes_accessed=4 * rows * (bin_count + rank_cols),
        ),
    )(flat, pair)


def gather_cells(cell_factor, early_work):
    outer = lax.axis_size("cell_outer")
    spread = jnp.broadcast_to(cell_factor[None], (outer,) + cell_factor.shape)
    mine = lax.all_to_all(spread, "cell_outer", 0, 0, tiled=True)
    mine, early = lax.optimization_barrier((mine, early_work()))
    if lax.axis_size("cell_core") == 1:
        return mine, None, early
    other = lax.ppermute(mine, "cell_core", [(0, 1), (1, 0)])
    return mine, other, early


def sweep_steps(a, first, count):
    n = a.shape[0]
    sub = lax.broadcasted_iota(jnp.int32, (n, n), 0)
    lane = lax.broadcasted_iota(jnp.int32, (n, n), 1)

    def step(s, a):
        k = first + s
        on_row = sub == k
        on_col = lane == k
        row = jnp.sum(jnp.where(on_row, a, 0.0), axis=0, keepdims=True)
        col = jnp.sum(jnp.where(on_col, a, 0.0), axis=1, keepdims=True)
        pivot = jnp.sum(jnp.where(on_col[:1], row, 0.0), axis=1, keepdims=True)
        inv = 1.0 / pivot
        scaled_row = row * inv
        upd = a - col * scaled_row
        upd = jnp.where(on_col, col * inv, upd)
        upd = jnp.where(on_row, scaled_row, upd)
        return jnp.where(on_row & on_col, -inv, upd)

    return lax.fori_loop(0, count, step, a, unroll=8)


def sweep_kernel(first, g_ref, o_ref):
    o_ref[...] = sweep_steps(g_ref[...], first, g_ref.shape[0] - first)


def sweep_rest(a, first):
    return pl.pallas_call(
        functools.partial(sweep_kernel, first),
        out_shape=jax.ShapeDtypeStruct(a.shape, jnp.float32),
    )(a)


def fused_kernel(core_ref, g_ref, pm_ref, po_ref, xm_ref, xo_ref, o_ref, m_ref, a_ref):
    o = pl.program_id(0)
    share = g_ref.shape[0] // (2 * pl.num_programs(0))

    @pl.when(o == 0)
    def _():
        a_ref[...] = g_ref[...]
        m_ref[...] = jnp.zeros_like(m_ref)

    a_ref[...] = sweep_steps(a_ref[...], o * share, share)
    m_ref[...] += jnp.sum(pm_ref[:, 0, 0] * xm_ref[...], axis=1) + jnp.sum(
        po_ref[:, 0, 0] * xo_ref[...], axis=1
    )
    o_ref[...] = a_ref[...]


def fused_half(gram, projected, mine, other, core):
    images, outer, _, rows, rank = projected.shape
    n = gram.shape[0]
    p_block = (images, 1, 1, rows, rank)
    grid_spec = pltpu.PrefetchScalarGridSpec(
        num_scalar_prefetch=1,
        grid=(outer,),
        in_specs=[
            pl.BlockSpec((n, n), lambda o, c: (0, 0)),
            pl.BlockSpec(p_block, lambda o, c: (0, o, c[0], 0, 0)),
            pl.BlockSpec(p_block, lambda o, c: (0, o, 1 - c[0], 0, 0)),
            pl.BlockSpec((1, rows, rank), lambda o, c: (o, 0, 0)),
            pl.BlockSpec((1, rows, rank), lambda o, c: (o, 0, 0)),
        ],
        out_specs=(
            pl.BlockSpec((n, n), lambda o, c: (0, 0)),
            pl.BlockSpec((images, rank), lambda o, c: (0, 0)),
        ),
        scratch_shapes=[pltpu.VMEM((n, n), jnp.float32)],
    )
    return pl.pallas_call(
        fused_kernel,
        out_shape=(
            jax.ShapeDtypeStruct(gram.shape, jnp.float32),
            jax.ShapeDtypeStruct((images, rank), jnp.float32),
        ),
        grid_spec=grid_spec,
    )(core, gram, projected, projected, mine, other)


def body(tensor, cell_factor, bin_factor):
    image_rows, cell_count, bin_count = tensor.shape
    rank_cols = bin_factor.shape[1]
    rows = image_rows * cell_count
    flat = tensor.reshape(rows, bin_count)
    gram_bin = exchange_sum(gram_of(bin_factor), "bin")
    mine, other, projected = gather_cells(
        cell_factor, lambda: project(flat, bin_factor, 0, rows)
    )
    outer, block_rows = mine.shape[:2]
    blocks = [mine] if other is None else [mine, other]
    gram_cell = sum(gram_of(b.reshape(-1, rank_cols)) for b in blocks)
    gram = gram_cell * gram_bin
    half = rank_cols // 2
    projected = projected.reshape(image_rows, outer, len(blocks), block_rows, rank_cols)
    if other is not None and half % outer == 0:
        core = lax.axis_index("cell_core").astype(jnp.int32).reshape(1)
        partial, mttkrp = fused_half(gram, projected, mine, other, core)
        neg_inv = sweep_rest(partial, half)
    else:
        if other is None:
            mttkrp = jnp.sum(projected[:, :, 0] * mine[None], axis=(1, 2))
        else:
            first = lax.axis_index("cell_core") == 0
            x0, x1 = jnp.where(first, mine, other), jnp.where(first, other, mine)
            mttkrp = jnp.sum(projected[:, :, 0] * x0[None], axis=(1, 2)) + jnp.sum(
                projected[:, :, 1] * x1[None], axis=(1, 2)
            )
        neg_inv = sweep_rest(gram, 0)
    totals = exchange_sum(mttkrp, "bin")
    own_cols = rank_cols // lax.axis_size("bin")
    own = lax.dynamic_slice_in_dim(neg_inv, lax.axis_index("bin") * own_cols, own_cols, 1)
    return -jnp.sum(totals[:, :, None] * own[None], axis=1)


def solution(mesh):
    cell_size, bin_size = mesh.shape["cell"], mesh.shape["bin"]
    core_count = 2 if cell_size % 2 == 0 else 1
    split = Mesh(
        mesh.devices.reshape(cell_size // core_count, core_count, bin_size),
        ("cell_outer", "cell_core", "bin"),
    )
    cell = ("cell_outer", "cell_core")
    placed = (P(cell, None, "bin"), P(cell, None), P("bin", None))
    return jax.shard_map(
        body, mesh=split, in_specs=placed, out_specs=P(cell, "bin"), check_vma=False
    )
```

```python
import functools

import jax
import jax.numpy as jnp
from jax import lax
from jax.experimental import pallas as pl
from jax.experimental.pallas import tpu as pltpu
from jax.sharding import Mesh, PartitionSpec as P


def exchange_sum(value, axis):
    size = lax.axis_size(axis)
    stride = 1
    while stride < size:
        pairs = [(i, i ^ stride) for i in range(size)]
        value = value + lax.ppermute(value, axis, pairs)
        stride *= 2
    return value


def split_pair(x):
    scaled = x * 65537.0
    hi = scaled - (scaled - x)
    lo = x - hi
    return hi.astype(jnp.bfloat16), lo.astype(jnp.bfloat16)


def gram_of(x):
    hi, lo = split_pair(x)
    both = jnp.concatenate([hi, lo], axis=1)
    full = lax.dot_general(
        both, both, (((0,), (0,)), ((), ())), preferred_element_type=jnp.float32
    )
    n = x.shape[1]
    return (full[:n, :n] + full[n:, n:]) + (full[:n, n:] + full[n:, :n])


def project_kernel(t_ref, b_ref, o_ref):
    rank_cols = o_ref.shape[1]
    hi, lo = split_pair(t_ref[...])
    pair = b_ref[...]
    acc = jnp.dot(hi, pair, preferred_element_type=jnp.float32)
    acc = acc + jnp.dot(lo, pair, preferred_element_type=jnp.float32)
    o_ref[...] = acc[:, :rank_cols] + acc[:, rank_cols:]


def project(flat, bin_factor, first_row, rows, block_rows=4096):
    bin_count = flat.shape[1]
    start = first_row // block_rows
    rank_cols = bin_factor.shape[1]
    b_hi, b_lo = split_pair(bin_factor)
    pair = jnp.concatenate([b_hi, b_lo], axis=1)
    return pl.pallas_call(
        project_kernel,
        out_shape=jax.ShapeDtypeStruct((rows, rank_cols), jnp.float32),
        grid=(rows // block_rows,),
        in_specs=[
            pl.BlockSpec((block_rows, bin_count), lambda i: (i + start, 0)),
            pl.BlockSpec((bin_count, 2 * rank_cols), lambda i: (0, 0)),
        ],
        out_specs=pl.BlockSpec((block_rows, rank_cols), lambda i: (i, 0)),
        cost_estimate=pl.CostEstimate(
            flops=8 * rows * bin_count * rank_cols,
            transcendentals=0,
            bytes_accessed=4 * rows * (bin_count + rank_cols),
        ),
    )(flat, pair)


def gather_cells(cell_factor, early_work):
    outer = lax.axis_size("cell_outer")
    spread = jnp.broadcast_to(cell_factor[None], (outer,) + cell_factor.shape)
    mine = lax.all_to_all(spread, "cell_outer", 0, 0, tiled=True)
    mine, early = lax.optimization_barrier((mine, early_work()))
    if lax.axis_size("cell_core") == 1:
        return mine, None, early
    other = lax.ppermute(mine, "cell_core", [(0, 1), (1, 0)])
    return mine, other, early


def sweep_steps(a, first, count):
    n = a.shape[0]
    sub = lax.broadcasted_iota(jnp.int32, (n, n), 0)
    lane = lax.broadcasted_iota(jnp.int32, (n, n), 1)

    def step(s, a):
        k = first + s
        on_row = sub == k
        on_col = lane == k
        row = jnp.sum(jnp.where(on_row, a, 0.0), axis=0, keepdims=True)
        col = jnp.sum(jnp.where(on_col, a, 0.0), axis=1, keepdims=True)
        pivot = jnp.sum(jnp.where(on_col[:1], row, 0.0), axis=1, keepdims=True)
        inv = 1.0 / pivot
        scaled_row = row * inv
        upd = a - col * scaled_row
        upd = jnp.where(on_col, col * inv, upd)
        upd = jnp.where(on_row, scaled_row, upd)
        return jnp.where(on_row & on_col, -inv, upd)

    return lax.fori_loop(0, count, step, a, unroll=8)


def sweep_kernel(first, g_ref, o_ref):
    o_ref[...] = -sweep_steps(g_ref[...], first, g_ref.shape[0] - first)


def sweep_rest(a, first):
    return pl.pallas_call(
        functools.partial(sweep_kernel, first),
        out_shape=jax.ShapeDtypeStruct(a.shape, jnp.float32),
    )(a)


def fused_kernel(core_ref, g_ref, pm_ref, po_ref, xm_ref, xo_ref, o_ref, m_ref, a_ref):
    o = pl.program_id(0)
    share = g_ref.shape[0] // (2 * pl.num_programs(0))

    @pl.when(o == 0)
    def _():
        a_ref[...] = g_ref[...]
        m_ref[...] = jnp.zeros_like(m_ref)

    a_ref[...] = sweep_steps(a_ref[...], o * share, share)
    m_ref[...] += jnp.sum(pm_ref[:, 0, 0] * xm_ref[...], axis=1) + jnp.sum(
        po_ref[:, 0, 0] * xo_ref[...], axis=1
    )
    o_ref[...] = a_ref[...]


def fused_half(gram, projected, mine, other, core):
    images, outer, _, rows, rank = projected.shape
    n = gram.shape[0]
    p_block = (images, 1, 1, rows, rank)
    grid_spec = pltpu.PrefetchScalarGridSpec(
        num_scalar_prefetch=1,
        grid=(outer,),
        in_specs=[
            pl.BlockSpec((n, n), lambda o, c: (0, 0)),
            pl.BlockSpec(p_block, lambda o, c: (0, o, c[0], 0, 0)),
            pl.BlockSpec(p_block, lambda o, c: (0, o, 1 - c[0], 0, 0)),
            pl.BlockSpec((1, rows, rank), lambda o, c: (o, 0, 0)),
            pl.BlockSpec((1, rows, rank), lambda o, c: (o, 0, 0)),
        ],
        out_specs=(
            pl.BlockSpec((n, n), lambda o, c: (0, 0)),
            pl.BlockSpec((images, rank), lambda o, c: (0, 0)),
        ),
        scratch_shapes=[pltpu.VMEM((n, n), jnp.float32)],
    )
    return pl.pallas_call(
        fused_kernel,
        out_shape=(
            jax.ShapeDtypeStruct(gram.shape, jnp.float32),
            jax.ShapeDtypeStruct((images, rank), jnp.float32),
        ),
        grid_spec=grid_spec,
    )(core, gram, projected, projected, mine, other)


def body(tensor, cell_factor, bin_factor):
    image_rows, cell_count, bin_count = tensor.shape
    rank_cols = bin_factor.shape[1]
    rows = image_rows * cell_count
    flat = tensor.reshape(rows, bin_count)
    gram_bin = exchange_sum(gram_of(bin_factor), "bin")
    mine, other, projected = gather_cells(
        cell_factor, lambda: project(flat, bin_factor, 0, rows)
    )
    outer, block_rows = mine.shape[:2]
    blocks = [mine] if other is None else [mine, other]
    gram_cell = sum(gram_of(b.reshape(-1, rank_cols)) for b in blocks)
    gram = gram_cell * gram_bin
    half = rank_cols // 2
    projected = projected.reshape(image_rows, outer, len(blocks), block_rows, rank_cols)
    if other is not None and half % outer == 0:
        core = lax.axis_index("cell_core").astype(jnp.int32).reshape(1)
        partial, mttkrp = fused_half(gram, projected, mine, other, core)
        inverse = sweep_rest(partial, half)
    else:
        if other is None:
            mttkrp = jnp.sum(projected[:, :, 0] * mine[None], axis=(1, 2))
        else:
            first = lax.axis_index("cell_core") == 0
            x0, x1 = jnp.where(first, mine, other), jnp.where(first, other, mine)
            mttkrp = jnp.sum(projected[:, :, 0] * x0[None], axis=(1, 2)) + jnp.sum(
                projected[:, :, 1] * x1[None], axis=(1, 2)
            )
        inverse = sweep_rest(gram, 0)
    totals = exchange_sum(mttkrp, "bin")
    own_cols = rank_cols // lax.axis_size("bin")
    own = lax.dynamic_slice_in_dim(inverse, lax.axis_index("bin") * own_cols, own_cols, 1)
    return jnp.sum(totals[:, :, None] * own[None], axis=1)


def solution(mesh):
    cell_size, bin_size = mesh.shape["cell"], mesh.shape["bin"]
    core_count = 2 if cell_size % 2 == 0 else 1
    split = Mesh(
        mesh.devices.reshape(cell_size // core_count, core_count, bin_size),
        ("cell_outer", "cell_core", "bin"),
    )
    cell = ("cell_outer", "cell_core")
    placed = (P(cell, None, "bin"), P(cell, None), P("bin", None))
    return jax.shard_map(
        body, mesh=split, in_specs=placed, out_specs=P(cell, "bin"), check_vma=False
    )
```

```python
import functools

import jax
import jax.numpy as jnp
from jax import lax
from jax.experimental import pallas as pl
from jax.experimental.pallas import tpu as pltpu
from jax.sharding import Mesh, PartitionSpec as P


def exchange_sum(value, axis):
    size = lax.axis_size(axis)
    stride = 1
    while stride < size:
        pairs = [(i, i ^ stride) for i in range(size)]
        value = value + lax.ppermute(value, axis, pairs)
        stride *= 2
    return value


def split_pair(x):
    scaled = x * 65537.0
    hi = scaled - (scaled - x)
    lo = x - hi
    return hi.astype(jnp.bfloat16), lo.astype(jnp.bfloat16)


def gram_of(x):
    hi, lo = split_pair(x)
    both = jnp.concatenate([hi, lo], axis=1)
    full = lax.dot_general(
        both, both, (((0,), (0,)), ((), ())), preferred_element_type=jnp.float32
    )
    n = x.shape[1]
    return (full[:n, :n] + full[n:, n:]) + (full[:n, n:] + full[n:, :n])


def project_kernel(t_ref, b_ref, o_ref):
    rank_cols = o_ref.shape[1]
    hi, lo = split_pair(t_ref[...])
    pair = b_ref[...]
    acc = jnp.dot(hi, pair, preferred_element_type=jnp.float32)
    acc = acc + jnp.dot(lo, pair, preferred_element_type=jnp.float32)
    o_ref[...] = acc[:, :rank_cols] + acc[:, rank_cols:]


def project(flat, bin_factor, first_row, rows, block_rows=4096):
    bin_count = flat.shape[1]
    start = first_row // block_rows
    rank_cols = bin_factor.shape[1]
    b_hi, b_lo = split_pair(bin_factor)
    pair = jnp.concatenate([b_hi, b_lo], axis=1)
    return pl.pallas_call(
        project_kernel,
        out_shape=jax.ShapeDtypeStruct((rows, rank_cols), jnp.float32),
        grid=(rows // block_rows,),
        in_specs=[
            pl.BlockSpec((block_rows, bin_count), lambda i: (i + start, 0)),
            pl.BlockSpec((bin_count, 2 * rank_cols), lambda i: (0, 0)),
        ],
        out_specs=pl.BlockSpec((block_rows, rank_cols), lambda i: (i, 0)),
        cost_estimate=pl.CostEstimate(
            flops=8 * rows * bin_count * rank_cols,
            transcendentals=0,
            bytes_accessed=4 * rows * (bin_count + rank_cols),
        ),
    )(flat, pair)


def gather_cells(cell_factor, early_work):
    outer = lax.axis_size("cell_outer")
    spread = jnp.broadcast_to(cell_factor[None], (outer,) + cell_factor.shape)
    mine = lax.all_to_all(spread, "cell_outer", 0, 0, tiled=True)
    mine, early = lax.optimization_barrier((mine, early_work()))
    if lax.axis_size("cell_core") == 1:
        return mine, None, early
    other = lax.ppermute(mine, "cell_core", [(0, 1), (1, 0)])
    return mine, other, early


def sweep_steps(a, first, count):
    n = a.shape[0]
    sub = lax.broadcasted_iota(jnp.int32, (n, n), 0)
    lane = lax.broadcasted_iota(jnp.int32, (n, n), 1)

    def step(s, a):
        k = first + s
        on_row = sub == k
        on_col = lane == k
        row = jnp.sum(jnp.where(on_row, a, 0.0), axis=0, keepdims=True)
        col = jnp.sum(jnp.where(on_col, a, 0.0), axis=1, keepdims=True)
        pivot = jnp.sum(jnp.where(on_col[:1], row, 0.0), axis=1, keepdims=True)
        inv = 1.0 / pivot
        scaled_row = row * inv
        upd = a - col * scaled_row
        upd = jnp.where(on_col, col * inv, upd)
        upd = jnp.where(on_row, scaled_row, upd)
        return jnp.where(on_row & on_col, -inv, upd)

    return lax.fori_loop(0, count, step, a, unroll=8)


def sweep_kernel(first, g_ref, o_ref):
    o_ref[...] = sweep_steps(g_ref[...], first, g_ref.shape[0] - first)


def sweep_rest(a, first):
    return pl.pallas_call(
        functools.partial(sweep_kernel, first),
        out_shape=jax.ShapeDtypeStruct(a.shape, jnp.float32),
    )(a)


def fused_kernel(core_ref, g_ref, pm_ref, po_ref, xm_ref, xo_ref, o_ref, m_ref, a_ref):
    o = pl.program_id(0)
    share = (3 * g_ref.shape[0] // 4) // pl.num_programs(0)

    @pl.when(o == 0)
    def _():
        a_ref[...] = g_ref[...]
        m_ref[...] = jnp.zeros_like(m_ref)

    a_ref[...] = sweep_steps(a_ref[...], o * share, share)
    m_ref[...] += jnp.sum(pm_ref[:, 0, 0] * xm_ref[...], axis=1) + jnp.sum(
        po_ref[:, 0, 0] * xo_ref[...], axis=1
    )
    o_ref[...] = a_ref[...]


def fused_half(gram, projected, mine, other, core):
    images, outer, _, rows, rank = projected.shape
    n = gram.shape[0]
    p_block = (images, 1, 1, rows, rank)
    grid_spec = pltpu.PrefetchScalarGridSpec(
        num_scalar_prefetch=1,
        grid=(outer,),
        in_specs=[
            pl.BlockSpec((n, n), lambda o, c: (0, 0)),
            pl.BlockSpec(p_block, lambda o, c: (0, o, c[0], 0, 0)),
            pl.BlockSpec(p_block, lambda o, c: (0, o, 1 - c[0], 0, 0)),
            pl.BlockSpec((1, rows, rank), lambda o, c: (o, 0, 0)),
            pl.BlockSpec((1, rows, rank), lambda o, c: (o, 0, 0)),
        ],
        out_specs=(
            pl.BlockSpec((n, n), lambda o, c: (0, 0)),
            pl.BlockSpec((images, rank), lambda o, c: (0, 0)),
        ),
        scratch_shapes=[pltpu.VMEM((n, n), jnp.float32)],
    )
    return pl.pallas_call(
        fused_kernel,
        out_shape=(
            jax.ShapeDtypeStruct(gram.shape, jnp.float32),
            jax.ShapeDtypeStruct((images, rank), jnp.float32),
        ),
        grid_spec=grid_spec,
    )(core, gram, projected, projected, mine, other)


def body(tensor, cell_factor, bin_factor):
    image_rows, cell_count, bin_count = tensor.shape
    rank_cols = bin_factor.shape[1]
    rows = image_rows * cell_count
    flat = tensor.reshape(rows, bin_count)
    gram_bin = exchange_sum(gram_of(bin_factor), "bin")
    mine, other, projected = gather_cells(
        cell_factor, lambda: project(flat, bin_factor, 0, rows)
    )
    outer, block_rows = mine.shape[:2]
    blocks = [mine] if other is None else [mine, other]
    gram_cell = sum(gram_of(b.reshape(-1, rank_cols)) for b in blocks)
    gram = gram_cell * gram_bin
    half = 3 * rank_cols // 4
    projected = projected.reshape(image_rows, outer, len(blocks), block_rows, rank_cols)
    if other is not None and half % outer == 0:
        core = lax.axis_index("cell_core").astype(jnp.int32).reshape(1)
        partial, mttkrp = fused_half(gram, projected, mine, other, core)
        neg_inv = sweep_rest(partial, half)
    else:
        if other is None:
            mttkrp = jnp.sum(projected[:, :, 0] * mine[None], axis=(1, 2))
        else:
            first = lax.axis_index("cell_core") == 0
            x0, x1 = jnp.where(first, mine, other), jnp.where(first, other, mine)
            mttkrp = jnp.sum(projected[:, :, 0] * x0[None], axis=(1, 2)) + jnp.sum(
                projected[:, :, 1] * x1[None], axis=(1, 2)
            )
        neg_inv = sweep_rest(gram, 0)
    totals = exchange_sum(mttkrp, "bin")
    own_cols = rank_cols // lax.axis_size("bin")
    own = lax.dynamic_slice_in_dim(neg_inv, lax.axis_index("bin") * own_cols, own_cols, 1)
    return -jnp.dot(totals, own, precision=lax.Precision.HIGHEST)


def solution(mesh):
    cell_size, bin_size = mesh.shape["cell"], mesh.shape["bin"]
    core_count = 2 if cell_size % 2 == 0 else 1
    split = Mesh(
        mesh.devices.reshape(cell_size // core_count, core_count, bin_size),
        ("cell_outer", "cell_core", "bin"),
    )
    cell = ("cell_outer", "cell_core")
    placed = (P(cell, None, "bin"), P(cell, None), P("bin", None))
    return jax.shard_map(
        body, mesh=split, in_specs=placed, out_specs=P(cell, "bin"), check_vma=False
    )
```

```python
import functools

import jax
import jax.numpy as jnp
from jax import lax
from jax.experimental import pallas as pl
from jax.experimental.pallas import tpu as pltpu
from jax.sharding import Mesh, PartitionSpec as P


def exchange_sum(value, axis):
    size = lax.axis_size(axis)
    stride = 1
    while stride < size:
        pairs = [(i, i ^ stride) for i in range(size)]
        value = value + lax.ppermute(value, axis, pairs)
        stride *= 2
    return value


def split_pair(x):
    scaled = x * 65537.0
    hi = scaled - (scaled - x)
    lo = x - hi
    return hi.astype(jnp.bfloat16), lo.astype(jnp.bfloat16)


def gram_of(x):
    hi, lo = split_pair(x)
    both = jnp.concatenate([hi, lo], axis=1)
    full = lax.dot_general(
        both, both, (((0,), (0,)), ((), ())), preferred_element_type=jnp.float32
    )
    n = x.shape[1]
    return (full[:n, :n] + full[n:, n:]) + (full[:n, n:] + full[n:, :n])


def project_kernel(t_ref, b_ref, o_ref):
    rank_cols = o_ref.shape[1]
    hi, lo = split_pair(t_ref[...])
    pair = b_ref[...]
    acc = jnp.dot(hi, pair, preferred_element_type=jnp.float32)
    acc = acc + jnp.dot(lo, pair, preferred_element_type=jnp.float32)
    o_ref[...] = acc[:, :rank_cols] + acc[:, rank_cols:]


def project(flat, bin_factor, first_row, rows, block_rows=4096):
    bin_count = flat.shape[1]
    start = first_row // block_rows
    rank_cols = bin_factor.shape[1]
    b_hi, b_lo = split_pair(bin_factor)
    pair = jnp.concatenate([b_hi, b_lo], axis=1)
    return pl.pallas_call(
        project_kernel,
        out_shape=jax.ShapeDtypeStruct((rows, rank_cols), jnp.float32),
        grid=(rows // block_rows,),
        in_specs=[
            pl.BlockSpec((block_rows, bin_count), lambda i: (i + start, 0)),
            pl.BlockSpec((bin_count, 2 * rank_cols), lambda i: (0, 0)),
        ],
        out_specs=pl.BlockSpec((block_rows, rank_cols), lambda i: (i, 0)),
        cost_estimate=pl.CostEstimate(
            flops=8 * rows * bin_count * rank_cols,
            transcendentals=0,
            bytes_accessed=4 * rows * (bin_count + rank_cols),
        ),
    )(flat, pair)


def gather_cells(cell_factor, early_work):
    outer = lax.axis_size("cell_outer")
    spread = jnp.broadcast_to(cell_factor[None], (outer,) + cell_factor.shape)
    mine = lax.all_to_all(spread, "cell_outer", 0, 0, tiled=True)
    mine, early = lax.optimization_barrier((mine, early_work()))
    if lax.axis_size("cell_core") == 1:
        return mine, None, early
    other = lax.ppermute(mine, "cell_core", [(0, 1), (1, 0)])
    return mine, other, early


def sweep_steps(a, first, count):
    n = a.shape[0]
    sub = lax.broadcasted_iota(jnp.int32, (n, n), 0)
    lane = lax.broadcasted_iota(jnp.int32, (n, n), 1)

    def step(s, a):
        k = first + s
        on_row = sub == k
        on_col = lane == k
        row = jnp.sum(jnp.where(on_row, a, 0.0), axis=0, keepdims=True)
        col = jnp.sum(jnp.where(on_col, a, 0.0), axis=1, keepdims=True)
        pivot = jnp.sum(jnp.where(on_col[:1], row, 0.0), axis=1, keepdims=True)
        inv = 1.0 / pivot
        scaled_row = row * inv
        upd = a - col * scaled_row
        upd = jnp.where(on_col, col * inv, upd)
        upd = jnp.where(on_row, scaled_row, upd)
        return jnp.where(on_row & on_col, -inv, upd)

    return lax.fori_loop(0, count, step, a, unroll=8)


def sweep_kernel(first, g_ref, o_ref):
    o_ref[...] = sweep_steps(g_ref[...], first, g_ref.shape[0] - first)


def sweep_rest(a, first):
    return pl.pallas_call(
        functools.partial(sweep_kernel, first),
        out_shape=jax.ShapeDtypeStruct(a.shape, jnp.float32),
    )(a)


def fused_kernel(core_ref, g_ref, pm_ref, po_ref, xm_ref, xo_ref, o_ref, m_ref, a_ref):
    o = pl.program_id(0)
    share = (7 * g_ref.shape[0] // 8) // pl.num_programs(0)

    @pl.when(o == 0)
    def _():
        a_ref[...] = g_ref[...]
        m_ref[...] = jnp.zeros_like(m_ref)

    a_ref[...] = sweep_steps(a_ref[...], o * share, share)
    m_ref[...] += jnp.sum(pm_ref[:, 0, 0] * xm_ref[...], axis=1) + jnp.sum(
        po_ref[:, 0, 0] * xo_ref[...], axis=1
    )
    o_ref[...] = a_ref[...]


def fused_half(gram, projected, mine, other, core):
    images, outer, _, rows, rank = projected.shape
    n = gram.shape[0]
    p_block = (images, 1, 1, rows, rank)
    grid_spec = pltpu.PrefetchScalarGridSpec(
        num_scalar_prefetch=1,
        grid=(outer,),
        in_specs=[
            pl.BlockSpec((n, n), lambda o, c: (0, 0)),
            pl.BlockSpec(p_block, lambda o, c: (0, o, c[0], 0, 0)),
            pl.BlockSpec(p_block, lambda o, c: (0, o, 1 - c[0], 0, 0)),
            pl.BlockSpec((1, rows, rank), lambda o, c: (o, 0, 0)),
            pl.BlockSpec((1, rows, rank), lambda o, c: (o, 0, 0)),
        ],
        out_specs=(
            pl.BlockSpec((n, n), lambda o, c: (0, 0)),
            pl.BlockSpec((images, rank), lambda o, c: (0, 0)),
        ),
        scratch_shapes=[pltpu.VMEM((n, n), jnp.float32)],
    )
    return pl.pallas_call(
        fused_kernel,
        out_shape=(
            jax.ShapeDtypeStruct(gram.shape, jnp.float32),
            jax.ShapeDtypeStruct((images, rank), jnp.float32),
        ),
        grid_spec=grid_spec,
    )(core, gram, projected, projected, mine, other)


def body(tensor, cell_factor, bin_factor):
    image_rows, cell_count, bin_count = tensor.shape
    rank_cols = bin_factor.shape[1]
    rows = image_rows * cell_count
    flat = tensor.reshape(rows, bin_count)
    gram_bin = exchange_sum(gram_of(bin_factor), "bin")
    mine, other, projected = gather_cells(
        cell_factor, lambda: project(flat, bin_factor, 0, rows)
    )
    outer, block_rows = mine.shape[:2]
    blocks = [mine] if other is None else [mine, other]
    gram_cell = sum(gram_of(b.reshape(-1, rank_cols)) for b in blocks)
    gram = gram_cell * gram_bin
    half = 7 * rank_cols // 8
    projected = projected.reshape(image_rows, outer, len(blocks), block_rows, rank_cols)
    if other is not None and half % outer == 0:
        core = lax.axis_index("cell_core").astype(jnp.int32).reshape(1)
        partial, mttkrp = fused_half(gram, projected, mine, other, core)
        neg_inv = sweep_rest(partial, half)
    else:
        if other is None:
            mttkrp = jnp.sum(projected[:, :, 0] * mine[None], axis=(1, 2))
        else:
            first = lax.axis_index("cell_core") == 0
            x0, x1 = jnp.where(first, mine, other), jnp.where(first, other, mine)
            mttkrp = jnp.sum(projected[:, :, 0] * x0[None], axis=(1, 2)) + jnp.sum(
                projected[:, :, 1] * x1[None], axis=(1, 2)
            )
        neg_inv = sweep_rest(gram, 0)
    totals = exchange_sum(mttkrp, "bin")
    own_cols = rank_cols // lax.axis_size("bin")
    own = lax.dynamic_slice_in_dim(neg_inv, lax.axis_index("bin") * own_cols, own_cols, 1)
    return -jnp.dot(totals, own, precision=lax.Precision.HIGHEST)


def solution(mesh):
    cell_size, bin_size = mesh.shape["cell"], mesh.shape["bin"]
    core_count = 2 if cell_size % 2 == 0 else 1
    split = Mesh(
        mesh.devices.reshape(cell_size // core_count, core_count, bin_size),
        ("cell_outer", "cell_core", "bin"),
    )
    cell = ("cell_outer", "cell_core")
    placed = (P(cell, None, "bin"), P(cell, None), P("bin", None))
    return jax.shard_map(
        body, mesh=split, in_specs=placed, out_specs=P(cell, "bin"), check_vma=False
    )
```

```python
import functools

import jax
import jax.numpy as jnp
from jax import lax
from jax.experimental import pallas as pl
from jax.experimental.pallas import tpu as pltpu
from jax.sharding import Mesh, PartitionSpec as P


def exchange_sum(value, axis):
    size = lax.axis_size(axis)
    stride = 1
    while stride < size:
        pairs = [(i, i ^ stride) for i in range(size)]
        value = value + lax.ppermute(value, axis, pairs)
        stride *= 2
    return value


def split_pair(x):
    scaled = x * 65537.0
    hi = scaled - (scaled - x)
    lo = x - hi
    return hi.astype(jnp.bfloat16), lo.astype(jnp.bfloat16)


def gram_of(x):
    hi, lo = split_pair(x)
    both = jnp.concatenate([hi, lo], axis=1)
    full = lax.dot_general(
        both, both, (((0,), (0,)), ((), ())), preferred_element_type=jnp.float32
    )
    n = x.shape[1]
    return (full[:n, :n] + full[n:, n:]) + (full[:n, n:] + full[n:, :n])


def project_kernel(t_ref, b_ref, o_ref):
    rank_cols = o_ref.shape[1]
    hi, lo = split_pair(t_ref[...])
    pair = b_ref[...]
    acc = jnp.dot(hi, pair, preferred_element_type=jnp.float32)
    acc = acc + jnp.dot(lo, pair, preferred_element_type=jnp.float32)
    o_ref[...] = acc[:, :rank_cols] + acc[:, rank_cols:]


def project(flat, bin_factor, first_row, rows, block_rows=4096):
    bin_count = flat.shape[1]
    start = first_row // block_rows
    rank_cols = bin_factor.shape[1]
    b_hi, b_lo = split_pair(bin_factor)
    pair = jnp.concatenate([b_hi, b_lo], axis=1)
    return pl.pallas_call(
        project_kernel,
        out_shape=jax.ShapeDtypeStruct((rows, rank_cols), jnp.float32),
        grid=(rows // block_rows,),
        in_specs=[
            pl.BlockSpec((block_rows, bin_count), lambda i: (i + start, 0)),
            pl.BlockSpec((bin_count, 2 * rank_cols), lambda i: (0, 0)),
        ],
        out_specs=pl.BlockSpec((block_rows, rank_cols), lambda i: (i, 0)),
        cost_estimate=pl.CostEstimate(
            flops=8 * rows * bin_count * rank_cols,
            transcendentals=0,
            bytes_accessed=4 * rows * (bin_count + rank_cols),
        ),
    )(flat, pair)


def gather_cells(cell_factor, early_work):
    outer = lax.axis_size("cell_outer")
    spread = jnp.broadcast_to(cell_factor[None], (outer,) + cell_factor.shape)
    mine = lax.all_to_all(spread, "cell_outer", 0, 0, tiled=True)
    mine, early = lax.optimization_barrier((mine, early_work()))
    if lax.axis_size("cell_core") == 1:
        return mine, None, early
    other = lax.ppermute(mine, "cell_core", [(0, 1), (1, 0)])
    return mine, other, early


def sweep_steps(a, first, count):
    n = a.shape[0]
    sub = lax.broadcasted_iota(jnp.int32, (n, n), 0)
    lane = lax.broadcasted_iota(jnp.int32, (n, n), 1)

    def step(s, a):
        k = first + s
        on_row = sub == k
        on_col = lane == k
        row = jnp.sum(jnp.where(on_row, a, 0.0), axis=0, keepdims=True)
        col = jnp.sum(jnp.where(on_col, a, 0.0), axis=1, keepdims=True)
        pivot = jnp.sum(jnp.where(on_col[:1], row, 0.0), axis=1, keepdims=True)
        inv = 1.0 / pivot
        scaled_row = row * inv
        upd = a - col * scaled_row
        upd = jnp.where(on_col, col * inv, upd)
        upd = jnp.where(on_row, scaled_row, upd)
        return jnp.where(on_row & on_col, -inv, upd)

    return lax.fori_loop(0, count, step, a, unroll=8)


def sweep_kernel(first, g_ref, o_ref):
    o_ref[...] = sweep_steps(g_ref[...], first, g_ref.shape[0] - first)


def sweep_rest(a, first):
    return pl.pallas_call(
        functools.partial(sweep_kernel, first),
        out_shape=jax.ShapeDtypeStruct(a.shape, jnp.float32),
    )(a)


def fused_kernel(core_ref, gc_ref, gb_ref, pm_ref, po_ref, xm_ref, xo_ref, o_ref, m_ref, a_ref):
    o = pl.program_id(0)
    share = (3 * gc_ref.shape[0] // 4) // pl.num_programs(0)

    @pl.when(o == 0)
    def _():
        a_ref[...] = gc_ref[...] * gb_ref[...]
        m_ref[...] = jnp.zeros_like(m_ref)

    a_ref[...] = sweep_steps(a_ref[...], o * share, share)
    m_ref[...] += jnp.sum(pm_ref[:, 0, 0] * xm_ref[...], axis=1) + jnp.sum(
        po_ref[:, 0, 0] * xo_ref[...], axis=1
    )
    o_ref[...] = a_ref[...]


def fused_half(gram_cell, gram_bin, projected, mine, other, core):
    images, outer, _, rows, rank = projected.shape
    n = gram_cell.shape[0]
    p_block = (images, 1, 1, rows, rank)
    grid_spec = pltpu.PrefetchScalarGridSpec(
        num_scalar_prefetch=1,
        grid=(outer,),
        in_specs=[
            pl.BlockSpec((n, n), lambda o, c: (0, 0)),
            pl.BlockSpec((n, n), lambda o, c: (0, 0)),
            pl.BlockSpec(p_block, lambda o, c: (0, o, c[0], 0, 0)),
            pl.BlockSpec(p_block, lambda o, c: (0, o, 1 - c[0], 0, 0)),
            pl.BlockSpec((1, rows, rank), lambda o, c: (o, 0, 0)),
            pl.BlockSpec((1, rows, rank), lambda o, c: (o, 0, 0)),
        ],
        out_specs=(
            pl.BlockSpec((n, n), lambda o, c: (0, 0)),
            pl.BlockSpec((images, rank), lambda o, c: (0, 0)),
        ),
        scratch_shapes=[pltpu.VMEM((n, n), jnp.float32)],
    )
    return pl.pallas_call(
        fused_kernel,
        out_shape=(
            jax.ShapeDtypeStruct(gram_cell.shape, jnp.float32),
            jax.ShapeDtypeStruct((images, rank), jnp.float32),
        ),
        grid_spec=grid_spec,
    )(core, gram_cell, gram_bin, projected, projected, mine, other)


def body(tensor, cell_factor, bin_factor):
    image_rows, cell_count, bin_count = tensor.shape
    rank_cols = bin_factor.shape[1]
    rows = image_rows * cell_count
    flat = tensor.reshape(rows, bin_count)
    gram_bin = exchange_sum(gram_of(bin_factor), "bin")
    mine, other, projected = gather_cells(
        cell_factor, lambda: project(flat, bin_factor, 0, rows)
    )
    outer, block_rows = mine.shape[:2]
    blocks = [mine] if other is None else [mine, other]
    gram_cell = sum(gram_of(b.reshape(-1, rank_cols)) for b in blocks)
    half = 3 * rank_cols // 4
    projected = projected.reshape(image_rows, outer, len(blocks), block_rows, rank_cols)
    if other is not None and half % outer == 0:
        core = lax.axis_index("cell_core").astype(jnp.int32).reshape(1)
        partial, mttkrp = fused_half(gram_cell, gram_bin, projected, mine, other, core)
        neg_inv = sweep_rest(partial, half)
    else:
        if other is None:
            mttkrp = jnp.sum(projected[:, :, 0] * mine[None], axis=(1, 2))
        else:
            first = lax.axis_index("cell_core") == 0
            x0, x1 = jnp.where(first, mine, other), jnp.where(first, other, mine)
            mttkrp = jnp.sum(projected[:, :, 0] * x0[None], axis=(1, 2)) + jnp.sum(
                projected[:, :, 1] * x1[None], axis=(1, 2)
            )
        neg_inv = sweep_rest(gram_cell * gram_bin, 0)
    totals = exchange_sum(mttkrp, "bin")
    own_cols = rank_cols // lax.axis_size("bin")
    own = lax.dynamic_slice_in_dim(neg_inv, lax.axis_index("bin") * own_cols, own_cols, 1)
    return -jnp.dot(totals, own, precision=lax.Precision.HIGHEST)


def solution(mesh):
    cell_size, bin_size = mesh.shape["cell"], mesh.shape["bin"]
    core_count = 2 if cell_size % 2 == 0 else 1
    split = Mesh(
        mesh.devices.reshape(cell_size // core_count, core_count, bin_size),
        ("cell_outer", "cell_core", "bin"),
    )
    cell = ("cell_outer", "cell_core")
    placed = (P(cell, None, "bin"), P(cell, None), P("bin", None))
    return jax.shard_map(
        body, mesh=split, in_specs=placed, out_specs=P(cell, "bin"), check_vma=False
    )
```

```python
import functools

import jax
import jax.numpy as jnp
from jax import lax
from jax.experimental import pallas as pl
from jax.experimental.pallas import tpu as pltpu
from jax.sharding import Mesh, PartitionSpec as P


def exchange_sum(value, axis):
    size = lax.axis_size(axis)
    stride = 1
    while stride < size:
        pairs = [(i, i ^ stride) for i in range(size)]
        value = value + lax.ppermute(value, axis, pairs)
        stride *= 2
    return value


def split_pair(x):
    scaled = x * 65537.0
    hi = scaled - (scaled - x)
    lo = x - hi
    return hi.astype(jnp.bfloat16), lo.astype(jnp.bfloat16)


def gram_of(x):
    hi, lo = split_pair(x)
    both = jnp.concatenate([hi, lo], axis=1)
    full = lax.dot_general(
        both, both, (((0,), (0,)), ((), ())), preferred_element_type=jnp.float32
    )
    n = x.shape[1]
    return (full[:n, :n] + full[n:, n:]) + (full[:n, n:] + full[n:, :n])


def project_kernel(t_ref, b_ref, o_ref):
    rank_cols = o_ref.shape[1]
    hi, lo = split_pair(t_ref[...])
    pair = b_ref[...]
    acc = jnp.dot(hi, pair, preferred_element_type=jnp.float32)
    acc = acc + jnp.dot(lo, pair, preferred_element_type=jnp.float32)
    o_ref[...] = acc[:, :rank_cols] + acc[:, rank_cols:]


def project(flat, bin_factor, first_row, rows, block_rows=4096):
    bin_count = flat.shape[1]
    start = first_row // block_rows
    rank_cols = bin_factor.shape[1]
    b_hi, b_lo = split_pair(bin_factor)
    pair = jnp.concatenate([b_hi, b_lo], axis=1)
    return pl.pallas_call(
        project_kernel,
        out_shape=jax.ShapeDtypeStruct((rows, rank_cols), jnp.float32),
        grid=(rows // block_rows,),
        in_specs=[
            pl.BlockSpec((block_rows, bin_count), lambda i: (i + start, 0)),
            pl.BlockSpec((bin_count, 2 * rank_cols), lambda i: (0, 0)),
        ],
        out_specs=pl.BlockSpec((block_rows, rank_cols), lambda i: (i, 0)),
        cost_estimate=pl.CostEstimate(
            flops=8 * rows * bin_count * rank_cols,
            transcendentals=0,
            bytes_accessed=4 * rows * (bin_count + rank_cols),
        ),
    )(flat, pair)


def gather_cells(cell_factor, early_work):
    outer = lax.axis_size("cell_outer")
    spread = jnp.broadcast_to(cell_factor[None], (outer,) + cell_factor.shape)
    mine = lax.all_to_all(spread, "cell_outer", 0, 0, tiled=True)
    mine, early = lax.optimization_barrier((mine, early_work()))
    if lax.axis_size("cell_core") == 1:
        return mine, None, early
    other = lax.ppermute(mine, "cell_core", [(0, 1), (1, 0)])
    return mine, other, early


def sweep_steps(a, first, count, unroll=8):
    n = a.shape[0]
    sub = lax.broadcasted_iota(jnp.int32, (n, n), 0)
    lane = lax.broadcasted_iota(jnp.int32, (n, n), 1)

    def step(s, a):
        k = first + s
        on_row = sub == k
        on_col = lane == k
        row = jnp.sum(jnp.where(on_row, a, 0.0), axis=0, keepdims=True)
        col = jnp.sum(jnp.where(on_col, a, 0.0), axis=1, keepdims=True)
        pivot = jnp.sum(jnp.where(on_col[:1], row, 0.0), axis=1, keepdims=True)
        inv = 1.0 / pivot
        scaled_row = row * inv
        upd = a - col * scaled_row
        upd = jnp.where(on_col, col * inv, upd)
        upd = jnp.where(on_row, scaled_row, upd)
        return jnp.where(on_row & on_col, -inv, upd)

    return lax.fori_loop(0, count, step, a, unroll=unroll)


def sweep_kernel(first, g_ref, o_ref):
    o_ref[...] = sweep_steps(g_ref[...], first, g_ref.shape[0] - first)


def sweep_rest(a, first):
    return pl.pallas_call(
        functools.partial(sweep_kernel, first),
        out_shape=jax.ShapeDtypeStruct(a.shape, jnp.float32),
    )(a)


def fused_kernel(core_ref, g_ref, pm_ref, po_ref, xm_ref, xo_ref, o_ref, m_ref, a_ref):
    o = pl.program_id(0)
    share = (3 * g_ref.shape[0] // 4) // pl.num_programs(0)

    @pl.when(o == 0)
    def _():
        a_ref[...] = g_ref[...]
        m_ref[...] = jnp.zeros_like(m_ref)

    a_ref[...] = sweep_steps(a_ref[...], o * share, share, unroll=share)
    m_ref[...] += jnp.sum(pm_ref[:, 0, 0] * xm_ref[...], axis=1) + jnp.sum(
        po_ref[:, 0, 0] * xo_ref[...], axis=1
    )
    o_ref[...] = a_ref[...]


def fused_half(gram, projected, mine, other, core):
    images, outer, _, rows, rank = projected.shape
    n = gram.shape[0]
    p_block = (images, 1, 1, rows, rank)
    grid_spec = pltpu.PrefetchScalarGridSpec(
        num_scalar_prefetch=1,
        grid=(outer,),
        in_specs=[
            pl.BlockSpec((n, n), lambda o, c: (0, 0)),
            pl.BlockSpec(p_block, lambda o, c: (0, o, c[0], 0, 0)),
            pl.BlockSpec(p_block, lambda o, c: (0, o, 1 - c[0], 0, 0)),
            pl.BlockSpec((1, rows, rank), lambda o, c: (o, 0, 0)),
            pl.BlockSpec((1, rows, rank), lambda o, c: (o, 0, 0)),
        ],
        out_specs=(
            pl.BlockSpec((n, n), lambda o, c: (0, 0)),
            pl.BlockSpec((images, rank), lambda o, c: (0, 0)),
        ),
        scratch_shapes=[pltpu.VMEM((n, n), jnp.float32)],
    )
    return pl.pallas_call(
        fused_kernel,
        out_shape=(
            jax.ShapeDtypeStruct(gram.shape, jnp.float32),
            jax.ShapeDtypeStruct((images, rank), jnp.float32),
        ),
        grid_spec=grid_spec,
    )(core, gram, projected, projected, mine, other)


def body(tensor, cell_factor, bin_factor):
    image_rows, cell_count, bin_count = tensor.shape
    rank_cols = bin_factor.shape[1]
    rows = image_rows * cell_count
    flat = tensor.reshape(rows, bin_count)
    gram_bin = exchange_sum(gram_of(bin_factor), "bin")
    mine, other, projected = gather_cells(
        cell_factor, lambda: project(flat, bin_factor, 0, rows)
    )
    outer, block_rows = mine.shape[:2]
    blocks = [mine] if other is None else [mine, other]
    gram_cell = sum(gram_of(b.reshape(-1, rank_cols)) for b in blocks)
    gram = gram_cell * gram_bin
    half = 3 * rank_cols // 4
    projected = projected.reshape(image_rows, outer, len(blocks), block_rows, rank_cols)
    if other is not None and half % outer == 0:
        core = lax.axis_index("cell_core").astype(jnp.int32).reshape(1)
        partial, mttkrp = fused_half(gram, projected, mine, other, core)
        neg_inv = sweep_rest(partial, half)
    else:
        if other is None:
            mttkrp = jnp.sum(projected[:, :, 0] * mine[None], axis=(1, 2))
        else:
            first = lax.axis_index("cell_core") == 0
            x0, x1 = jnp.where(first, mine, other), jnp.where(first, other, mine)
            mttkrp = jnp.sum(projected[:, :, 0] * x0[None], axis=(1, 2)) + jnp.sum(
                projected[:, :, 1] * x1[None], axis=(1, 2)
            )
        neg_inv = sweep_rest(gram, 0)
    totals = exchange_sum(mttkrp, "bin")
    own_cols = rank_cols // lax.axis_size("bin")
    own = lax.dynamic_slice_in_dim(neg_inv, lax.axis_index("bin") * own_cols, own_cols, 1)
    return -jnp.dot(totals, own, precision=lax.Precision.HIGHEST)


def solution(mesh):
    cell_size, bin_size = mesh.shape["cell"], mesh.shape["bin"]
    core_count = 2 if cell_size % 2 == 0 else 1
    split = Mesh(
        mesh.devices.reshape(cell_size // core_count, core_count, bin_size),
        ("cell_outer", "cell_core", "bin"),
    )
    cell = ("cell_outer", "cell_core")
    placed = (P(cell, None, "bin"), P(cell, None), P("bin", None))
    return jax.shard_map(
        body, mesh=split, in_specs=placed, out_specs=P(cell, "bin"), check_vma=False
    )
```

```python
import functools

import jax
import jax.numpy as jnp
from jax import lax
from jax.experimental import pallas as pl
from jax.experimental.pallas import tpu as pltpu
from jax.sharding import Mesh, PartitionSpec as P


def exchange_sum(value, axis):
    size = lax.axis_size(axis)
    stride = 1
    while stride < size:
        pairs = [(i, i ^ stride) for i in range(size)]
        value = value + lax.ppermute(value, axis, pairs)
        stride *= 2
    return value


def split_pair(x):
    scaled = x * 65537.0
    hi = scaled - (scaled - x)
    lo = x - hi
    return hi.astype(jnp.bfloat16), lo.astype(jnp.bfloat16)


def gram_of(x):
    hi, lo = split_pair(x)
    both = jnp.concatenate([hi, lo], axis=1)
    full = lax.dot_general(
        both, both, (((0,), (0,)), ((), ())), preferred_element_type=jnp.float32
    )
    n = x.shape[1]
    return (full[:n, :n] + full[n:, n:]) + (full[:n, n:] + full[n:, :n])


def project_kernel(t_ref, b_ref, o_ref):
    rank_cols = o_ref.shape[1]
    hi, lo = split_pair(t_ref[...])
    pair = b_ref[...]
    acc = jnp.dot(hi, pair, preferred_element_type=jnp.float32)
    acc = acc + jnp.dot(lo, pair, preferred_element_type=jnp.float32)
    o_ref[...] = acc[:, :rank_cols] + acc[:, rank_cols:]


def project(flat, bin_factor, first_row, rows, block_rows=4096):
    bin_count = flat.shape[1]
    start = first_row // block_rows
    rank_cols = bin_factor.shape[1]
    b_hi, b_lo = split_pair(bin_factor)
    pair = jnp.concatenate([b_hi, b_lo], axis=1)
    return pl.pallas_call(
        project_kernel,
        out_shape=jax.ShapeDtypeStruct((rows, rank_cols), jnp.float32),
        grid=(rows // block_rows,),
        in_specs=[
            pl.BlockSpec((block_rows, bin_count), lambda i: (i + start, 0)),
            pl.BlockSpec((bin_count, 2 * rank_cols), lambda i: (0, 0)),
        ],
        out_specs=pl.BlockSpec((block_rows, rank_cols), lambda i: (i, 0)),
        cost_estimate=pl.CostEstimate(
            flops=8 * rows * bin_count * rank_cols,
            transcendentals=0,
            bytes_accessed=4 * rows * (bin_count + rank_cols),
        ),
    )(flat, pair)


def gather_cells(cell_factor, early_work):
    outer = lax.axis_size("cell_outer")
    spread = jnp.broadcast_to(cell_factor[None], (outer,) + cell_factor.shape)
    mine = lax.all_to_all(spread, "cell_outer", 0, 0, tiled=True)
    mine, early = lax.optimization_barrier((mine, early_work()))
    if lax.axis_size("cell_core") == 1:
        return mine, None, early
    other = lax.ppermute(mine, "cell_core", [(0, 1), (1, 0)])
    return mine, other, early


def sweep_steps(a, first, count, unroll=8):
    n = a.shape[0]
    sub = lax.broadcasted_iota(jnp.int32, (n, n), 0)
    lane = lax.broadcasted_iota(jnp.int32, (n, n), 1)

    def step(s, a):
        k = first + s
        on_row = sub == k
        on_col = lane == k
        row = jnp.sum(jnp.where(on_row, a, 0.0), axis=0, keepdims=True)
        col = jnp.sum(jnp.where(on_col, a, 0.0), axis=1, keepdims=True)
        pivot = jnp.sum(jnp.where(on_col[:1], row, 0.0), axis=1, keepdims=True)
        inv = 1.0 / pivot
        scaled_row = row * inv
        upd = a - col * scaled_row
        upd = jnp.where(on_col, col * inv, upd)
        upd = jnp.where(on_row, scaled_row, upd)
        return jnp.where(on_row & on_col, -inv, upd)

    return lax.fori_loop(0, count, step, a, unroll=unroll)


def sweep_kernel(first, g_ref, o_ref):
    count = g_ref.shape[0] - first
    o_ref[...] = sweep_steps(g_ref[...], first, count, unroll=min(count, 32))


def sweep_rest(a, first):
    return pl.pallas_call(
        functools.partial(sweep_kernel, first),
        out_shape=jax.ShapeDtypeStruct(a.shape, jnp.float32),
    )(a)


def fused_kernel(core_ref, g_ref, pm_ref, po_ref, xm_ref, xo_ref, o_ref, m_ref, a_ref):
    o = pl.program_id(0)
    share = (3 * g_ref.shape[0] // 4) // pl.num_programs(0)

    @pl.when(o == 0)
    def _():
        a_ref[...] = g_ref[...]
        m_ref[...] = jnp.zeros_like(m_ref)

    a_ref[...] = sweep_steps(a_ref[...], o * share, share, unroll=share)
    m_ref[...] += jnp.sum(pm_ref[:, 0, 0] * xm_ref[...], axis=1) + jnp.sum(
        po_ref[:, 0, 0] * xo_ref[...], axis=1
    )
    o_ref[...] = a_ref[...]


def fused_half(gram, projected, mine, other, core):
    images, outer, _, rows, rank = projected.shape
    n = gram.shape[0]
    p_block = (images, 1, 1, rows, rank)
    grid_spec = pltpu.PrefetchScalarGridSpec(
        num_scalar_prefetch=1,
        grid=(outer,),
        in_specs=[
            pl.BlockSpec((n, n), lambda o, c: (0, 0)),
            pl.BlockSpec(p_block, lambda o, c: (0, o, c[0], 0, 0)),
            pl.BlockSpec(p_block, lambda o, c: (0, o, 1 - c[0], 0, 0)),
            pl.BlockSpec((1, rows, rank), lambda o, c: (o, 0, 0)),
            pl.BlockSpec((1, rows, rank), lambda o, c: (o, 0, 0)),
        ],
        out_specs=(
            pl.BlockSpec((n, n), lambda o, c: (0, 0)),
            pl.BlockSpec((images, rank), lambda o, c: (0, 0)),
        ),
        scratch_shapes=[pltpu.VMEM((n, n), jnp.float32)],
    )
    return pl.pallas_call(
        fused_kernel,
        out_shape=(
            jax.ShapeDtypeStruct(gram.shape, jnp.float32),
            jax.ShapeDtypeStruct((images, rank), jnp.float32),
        ),
        grid_spec=grid_spec,
    )(core, gram, projected, projected, mine, other)


def body(tensor, cell_factor, bin_factor):
    image_rows, cell_count, bin_count = tensor.shape
    rank_cols = bin_factor.shape[1]
    rows = image_rows * cell_count
    flat = tensor.reshape(rows, bin_count)
    gram_bin = exchange_sum(gram_of(bin_factor), "bin")
    mine, other, projected = gather_cells(
        cell_factor, lambda: project(flat, bin_factor, 0, rows)
    )
    outer, block_rows = mine.shape[:2]
    blocks = [mine] if other is None else [mine, other]
    gram_cell = sum(gram_of(b.reshape(-1, rank_cols)) for b in blocks)
    gram = gram_cell * gram_bin
    half = 3 * rank_cols // 4
    projected = projected.reshape(image_rows, outer, len(blocks), block_rows, rank_cols)
    if other is not None and half % outer == 0:
        core = lax.axis_index("cell_core").astype(jnp.int32).reshape(1)
        partial, mttkrp = fused_half(gram, projected, mine, other, core)
        neg_inv = sweep_rest(partial, half)
    else:
        if other is None:
            mttkrp = jnp.sum(projected[:, :, 0] * mine[None], axis=(1, 2))
        else:
            first = lax.axis_index("cell_core") == 0
            x0, x1 = jnp.where(first, mine, other), jnp.where(first, other, mine)
            mttkrp = jnp.sum(projected[:, :, 0] * x0[None], axis=(1, 2)) + jnp.sum(
                projected[:, :, 1] * x1[None], axis=(1, 2)
            )
        neg_inv = sweep_rest(gram, 0)
    totals = exchange_sum(mttkrp, "bin")
    own_cols = rank_cols // lax.axis_size("bin")
    own = lax.dynamic_slice_in_dim(neg_inv, lax.axis_index("bin") * own_cols, own_cols, 1)
    return -jnp.dot(totals, own, precision=lax.Precision.HIGHEST)


def solution(mesh):
    cell_size, bin_size = mesh.shape["cell"], mesh.shape["bin"]
    core_count = 2 if cell_size % 2 == 0 else 1
    split = Mesh(
        mesh.devices.reshape(cell_size // core_count, core_count, bin_size),
        ("cell_outer", "cell_core", "bin"),
    )
    cell = ("cell_outer", "cell_core")
    placed = (P(cell, None, "bin"), P(cell, None), P("bin", None))
    return jax.shard_map(
        body, mesh=split, in_specs=placed, out_specs=P(cell, "bin"), check_vma=False
    )
```
